512 devices in a mesh: grp: 64 (over z_hi, y, core), mdl: 8 (over z_lo, x).
Axes of the slice: x: 4, y: 8, z: 8 (z_hi: 4, z_lo: 2; z = z_hi * 2 + z_lo), core: 2. Of those that a mesh axis runs over, the one named last changes fastest.
Arguments:
- draft_hidden: bfloat16 [128, 32, 2048], P('grp', None, 'mdl'), may hold values from -6 to 6
- q_weight: bfloat16 [4, 2048, 1024], P(None, None, 'mdl'), may hold values from -0.125 to 0.125
- kv_weight: bfloat16 [2, 2048, 1024], P(None, None, 'mdl'), may hold values from -0.125 to 0.125
- router_weight: float32 [2048, 4], replicated, may hold values from -0.125 to 0.125
- routes: int32 [128, 32, 2], P('grp'), may hold values from 0 to 3, all different within a row
- tree_mask: int32 [128, 32, 32], P('grp'), may hold values from 0 to 1, as said below
- accepted: int32 [128, 8], P('grp'), may hold values from 0 to 31, as said below
- cache_kv: bfloat16 [192, 2, 1024, 1024], P('grp', None, None, 'mdl')
- cache_len: int32 [192], P('grp'), may hold values from 1 to 1024
- slot_request: int32 [192], replicated, may hold values from 0 to 127, as said below
Outputs:
- verified: bfloat16 [128, 8, 2, 1024], P('grp', None, None, 'mdl')
The draws below stay inside these ranges and needn't reach their ends.
Inputs may be any that keep to these rules, and one draw needn't show every extreme that they name: `routes`: the 2 experts of one token differ. tree_mask[r, i, j] is 1 exactly when draft j is draft i or an ancestor of it; every draft's parent has a lower index and draft 0 is the root. `accepted`: each row holds the first 8 drafts of the root-to-node chain of one draft, in increasing order; a shorter chain is followed by repeats of its last draft. `slot_request`: the requests of one index of grp are the 2 in a row that it holds; they are served by 3 slots in all, 1 of them by two slots and the others by one; no index of grp holds more than 1 slot serving requests of any one index of grp, and some pairs of indices have exactly 1 such slot.
All inputs are finite; a program needn't handle non-finite values.
Results may differ from the reference program's by a relative error of at most 0.014.
The reference program's roundings to bfloat16 on the way count: a program that leaves them out, or rounds other values in their place, can miss the bound.
Values may be sent and summed in bfloat16 or wider, within the bound.
No kernel may reach another device: no remote copies, remote signals or barrier semaphores. Data moves between devices by JAX's collectives and lax.ppermute only.
A program may use at most 64 MiB of HBM per device.

```python
import jax
import jax.numpy as jnp
from jax import lax

D = 2048
HEAD_SIZE = 128
KEY_VALUE_HEADS = 8
AEXP = 4
TOPK = 2
DRAFT = 32
ACC = 8
REQUESTS_PER_GRP = 2
CACHE_PER_SLOT = 1024
SLOTS = 3
REQS = 128
TOTAL_SLOTS = 192


def tree_tables(key):
    tree_key = jax.random.fold_in(key, 11)
    positions = jnp.arange(DRAFT, dtype=jnp.int32)
    highest = jnp.maximum(positions, 1)
    parent = jax.random.randint(tree_key, (REQS, DRAFT), 0, highest[None, :])
    same_node = positions[None, None, :] == positions[None, :, None]
    parent_link = (positions[None, None, :] == parent[:, :, None]) & (positions[None, :, None] > 0)
    reached = (same_node | parent_link).astype(jnp.int32)
    for squaring in range(DRAFT.bit_length()):
        reached = jnp.minimum(jnp.matmul(reached, reached), 1)
    target = jax.random.randint(jax.random.fold_in(tree_key, 1), (REQS,), 0, DRAFT)
    target = target.at[0].set(DRAFT - 1)
    ancestry = jnp.take_along_axis(reached, target[:, None, None], axis=1)[:, 0, :]
    ordinal = jnp.cumsum(ancestry, axis=1) - 1
    chain_len = jnp.sum(ancestry, axis=1)
    places = jnp.arange(ACC, dtype=jnp.int32)
    matched = (ancestry[:, None, :] == 1) & (ordinal[:, None, :] == places[None, :, None])
    picked = jnp.sum(jnp.where(matched, positions[None, None, :], 0), axis=2)
    accepted_rows = jnp.where(places[None, :] < chain_len[:, None], picked, target[:, None])
    return (reached.astype(jnp.int32), accepted_rows.astype(jnp.int32))


def draw_tree_mask(key, part):
    return tree_tables(key)[0]


def draw_accepted(key, part):
    return tree_tables(key)[1]


def draw_cache_kv(key, part):
    table_entries = jax.random.normal(jax.random.fold_in(key, 21), (TOTAL_SLOTS, 2, CACHE_PER_SLOT, KEY_VALUE_HEADS * HEAD_SIZE), jnp.float32)
    return table_entries.astype(jnp.bfloat16)


def draw_cache_len(key, part):
    length_values = jax.random.randint(jax.random.fold_in(key, 31), (TOTAL_SLOTS,), 1, CACHE_PER_SLOT + 1)
    longest_length = jax.random.randint(jax.random.fold_in(key, 32), (), 0, TOTAL_SLOTS)
    return length_values.at[longest_length].set(CACHE_PER_SLOT).astype(jnp.int32)


def draw_slot_request(key, part):
    groups = REQS // REQUESTS_PER_GRP
    base_key = jax.random.fold_in(key, 41)
    first_order = jax.random.permutation(jax.random.fold_in(base_key, 1), groups).astype(jnp.int32)
    second_order = jax.random.permutation(jax.random.fold_in(base_key, 2), groups).astype(jnp.int32)
    column = jnp.arange(SLOTS, dtype=jnp.int32)
    home_lookup = second_order[(first_order[:, None] + column[None, :]) % groups]
    split_keys = jax.random.split(jax.random.fold_in(base_key, 3), groups)
    doubled = jax.vmap(lambda one_key: jax.random.permutation(one_key, REQUESTS_PER_GRP))(split_keys).astype(jnp.int32)
    singles = jnp.broadcast_to(jnp.arange(REQUESTS_PER_GRP, dtype=jnp.int32)[None, :], (groups, REQUESTS_PER_GRP))
    pieces = jnp.concatenate([singles, doubled[:, :REQUESTS_PER_GRP // 2]], axis=1)
    order_keys = jax.random.split(jax.random.fold_in(base_key, 4), groups)
    orders = jax.vmap(lambda one_key: jax.random.permutation(one_key, SLOTS))(order_keys).astype(jnp.int32)
    shuffled = jnp.take_along_axis(pieces, orders, axis=1)
    nearby_rows = shuffled[home_lookup, column[None, :]]
    return (home_lookup * REQUESTS_PER_GRP + nearby_rows).reshape(TOTAL_SLOTS).astype(jnp.int32)


def level_of(key, extent, shards, least, high):
    def one(dim, blocks):
        heights = jax.random.uniform(jax.random.fold_in(jax.random.fold_in(key, 6), dim), (blocks,), jnp.float32, least / len(shards), high / len(shards))
        return jnp.repeat(jnp.exp(heights), extent[dim] // blocks).reshape((-1,) + (1,) * (len(extent) - dim - 1))

    gain = one(*shards[0])
    for cut in shards[1:]:
        gain = gain * one(*cut)
    return gain


def choose_distinct(stream_key, rows, number_of, top, lift):
    order = jax.random.permutation(jax.random.fold_in(stream_key, 1), number_of)
    pull = order
    for power in range(3):
        pull = pull * pull // number_of
    pull = pull * lift // number_of
    lots = jax.random.randint(jax.random.fold_in(stream_key, 2), (rows, number_of), 0, 4096) + pull
    sure = jax.random.permutation(jax.random.fold_in(stream_key, 3), rows)[jnp.arange(number_of) % rows]
    lots = jnp.where(jnp.arange(rows)[:, None] == sure[None, :], 1 << 14, lots)
    merit = lots * number_of + jnp.arange(number_of)
    return lax.top_k(merit.astype(jnp.int32), top)[1].astype(jnp.int32)


def noise(stream_key, shape, scale, bound, shards=(), kind=jnp.bfloat16):
    level = level_of(stream_key, shape, shards, -0.22, 0.18) if shards else 1.0
    drawn = jax.random.normal(stream_key, shape, jnp.float32) * scale * level
    return jnp.minimum(jnp.maximum(drawn, -bound), bound).astype(kind)


def setup_inputs(seed: int = 0) -> dict:
    key_of = jax.random.split(jax.random.key(seed), 11)
    draft_hidden = noise(key_of[0], (REQS, DRAFT, D), 1.0, 6.0, ((0, 64), (2, 8)))
    q_weight = noise(key_of[1], (AEXP, D, KEY_VALUE_HEADS * HEAD_SIZE), D ** -0.5, 0.125, ((2, 8),))
    kv_weight = noise(key_of[2], (2, D, KEY_VALUE_HEADS * HEAD_SIZE), D ** -0.5, 0.125, ((2, 8),))
    router_weight = noise(key_of[3], (D, AEXP), D ** -0.5, 0.125, (), jnp.float32)
    routes = choose_distinct(key_of[4], REQS * DRAFT, AEXP, TOPK, 4096).reshape((REQS, DRAFT, TOPK))
    tree_mask = draw_tree_mask(jax.random.fold_in(key_of[10], 71), 0)
    accepted = draw_accepted(jax.random.fold_in(key_of[10], 71), 0)
    cache_kv = draw_cache_kv(jax.random.fold_in(key_of[10], 71), 0)
    cache_len = draw_cache_len(jax.random.fold_in(key_of[10], 71), 0)
    slot_request = draw_slot_request(jax.random.fold_in(key_of[10], 71), 0)
    return {"draft_hidden": draft_hidden, "q_weight": q_weight, "kv_weight": kv_weight, "router_weight": router_weight, "routes": routes, "tree_mask": tree_mask, "accepted": accepted, "cache_kv": cache_kv, "cache_len": cache_len, "slot_request": slot_request}


def softmax_piece(scores, usable, values, contract):
    masked = jnp.where(usable, scores, -jnp.inf)
    peak_score = jnp.max(masked, axis=-1)
    weights_low = jnp.exp(masked - peak_score[..., None]).astype(jnp.bfloat16)
    weights_full = weights_low.astype(jnp.float32)
    denominator = jnp.sum(weights_full, axis=-1)
    numerator = jnp.einsum(contract, weights_full, values, precision=lax.Precision.HIGHEST)
    return peak_score, denominator, numerator


def reference(draft_hidden, q_weight, kv_weight, router_weight, routes, tree_mask, accepted, cache_kv, cache_len, slot_request):
    highest = lax.Precision.HIGHEST
    score_scale = HEAD_SIZE ** -0.5
    token_count = REQS * DRAFT
    flattened = draft_hidden.reshape(token_count, D).astype(jnp.float32)
    all_queries = jnp.einsum("nd,edw->new", flattened, q_weight.astype(jnp.float32), precision=highest)
    projected_kv = jnp.einsum("nd,cdw->ncw", flattened, kv_weight.astype(jnp.float32), precision=highest)
    logits = jnp.dot(flattened, router_weight, precision=highest)
    route_flat = routes.reshape(token_count, TOPK)
    chosen = jnp.take_along_axis(logits, route_flat, axis=1)
    gate_probs = jax.nn.softmax(chosen, axis=-1).reshape(REQS, DRAFT, TOPK)
    queries = jnp.take_along_axis(all_queries, route_flat[:, :, None], axis=1).astype(jnp.bfloat16)
    queries = queries.reshape(REQS, DRAFT, TOPK, KEY_VALUE_HEADS, HEAD_SIZE).astype(jnp.float32)
    draft_keys = projected_kv[:, 0].astype(jnp.bfloat16).reshape(REQS, DRAFT, KEY_VALUE_HEADS, HEAD_SIZE).astype(jnp.float32)
    draft_values = projected_kv[:, 1].astype(jnp.bfloat16).reshape(REQS, DRAFT, KEY_VALUE_HEADS, HEAD_SIZE).astype(jnp.float32)
    tree_scores = jnp.einsum("rqkhd,rjhd->rqkhj", queries, draft_keys, precision=highest) * score_scale
    allowed = (tree_mask > 0)[:, :, None, None, :]
    tree_peak, tree_den, tree_num = softmax_piece(tree_scores, allowed, draft_values, "rqkhj,rjhd->rqkhd")
    positions = jnp.arange(CACHE_PER_SLOT, dtype=jnp.int32)

    def slot_piece(packed):
        owner, length, stored = packed
        slot_queries = queries[owner]
        stored_full = stored.astype(jnp.float32).reshape(2, CACHE_PER_SLOT, KEY_VALUE_HEADS, HEAD_SIZE)
        scores = jnp.einsum("qkhd,chd->qkhc", slot_queries, stored_full[0], precision=highest) * score_scale
        return softmax_piece(scores, positions < length, stored_full[1], "qkhc,chd->qkhd")

    slot_peak, slot_den, slot_num = lax.map(slot_piece, (slot_request, cache_len, cache_kv))
    matched = jnp.arange(REQS, dtype=jnp.int32)[:, None] == slot_request[None, :]
    candidate = jnp.where(matched[:, :, None, None, None], slot_peak[None], -jnp.inf)
    running_max = jnp.maximum(tree_peak, jnp.max(candidate, axis=1))
    rescale = jnp.exp(tree_peak - running_max)
    weight = jnp.exp(candidate - running_max[:, None])
    denominator = tree_den * rescale + jnp.sum(weight * slot_den[None], axis=1)
    numerator = tree_num * rescale[..., None] + jnp.einsum("rnqkh,nqkhd->rqkhd", weight, slot_num, precision=highest)
    mixed = gate_probs[:, :, :, None, None] * numerator / denominator[..., None]
    picked = jnp.take_along_axis(mixed, accepted[:, :, None, None, None], axis=1)
    return picked.reshape(REQS, ACC, TOPK, KEY_VALUE_HEADS * HEAD_SIZE).astype(jnp.bfloat16)
```

```python
import jax
import jax.numpy as jnp
from jax import lax
from jax.sharding import PartitionSpec as P

HEAD_SIZE = 128


def softmax_piece(scores, usable, values, contract):
    masked = jnp.where(usable, scores, -jnp.inf)
    peak_score = jnp.max(masked, axis=-1)
    weights_low = jnp.exp(masked - peak_score[..., None]).astype(jnp.bfloat16)
    denominator = jnp.sum(weights_low.astype(jnp.float32), axis=-1)
    numerator = jnp.einsum(contract, weights_low, values, preferred_element_type=jnp.float32)
    return (peak_score, denominator, numerator)


def on_device(
    draft_hidden,
    q_weight,
    kv_weight,
    router_weight,
    routes,
    tree_mask,
    accepted,
    cache_kv,
    cache_len,
    slot_request,
):
    highest = lax.Precision.HIGHEST
    requests, drafts, part_width = draft_hidden.shape
    experts = q_weight.shape[0]
    head_width = q_weight.shape[2]
    head_count = head_width // HEAD_SIZE
    topk_count = routes.shape[2]
    kept_rows = accepted.shape[1]
    score_scale = HEAD_SIZE ** (-0.5)
    group_count = lax.axis_size("grp")
    group_idx = lax.axis_index("grp")
    slot_count = cache_kv.shape[0]
    cache_size = cache_kv.shape[2]

    hidden = lax.all_gather(draft_hidden, "mdl", axis=2, tiled=True)
    acc_hidden = jnp.take_along_axis(hidden, accepted[:, :, None], axis=1)
    acc_routes = jnp.take_along_axis(routes, accepted[:, :, None], axis=1)
    acc_mask = jnp.take_along_axis(tree_mask, accepted[:, :, None], axis=1)

    q_sum = jnp.einsum("rad,edw->raew", acc_hidden, q_weight, preferred_element_type=jnp.float32)
    kv_sum = jnp.einsum("rtd,cdw->rtcw", hidden, kv_weight, preferred_element_type=jnp.float32)
    logit_sum = jnp.einsum(
        "rad,de->rae", acc_hidden.astype(jnp.float32), router_weight, precision=highest
    )
    chosen_mask = acc_routes[..., None] == jnp.arange(experts, dtype=jnp.int32)
    chosen = jnp.sum(jnp.where(chosen_mask, logit_sum[:, :, None, :], 0.0), axis=3)
    gate_probs = jax.nn.softmax(chosen, axis=-1)
    queries = jnp.sum(jnp.where(chosen_mask[..., None], q_sum[:, :, None], 0.0), axis=3)
    queries = queries.astype(jnp.bfloat16)
    draft_keys = kv_sum[:, :, 0].astype(jnp.bfloat16)
    draft_values = kv_sum[:, :, 1].astype(jnp.bfloat16)

    tree_scores = (
        jnp.einsum("rakw,rjw->rakj", queries, draft_keys, preferred_element_type=jnp.float32)
        * score_scale
    )
    tree_peak, tree_den, tree_num = softmax_piece(
        tree_scores, (acc_mask > 0)[:, :, None, :], draft_values, "rakj,rjw->rakw"
    )

    slot_table = slot_request.reshape(group_count, slot_count)
    home_of = slot_table // requests
    local_of = slot_table % requests
    mine = home_of == group_idx
    picked = jnp.sum(jnp.where(mine, local_of, 0), axis=1)
    any_mine = jnp.any(mine, axis=1)
    outgoing = jnp.where(any_mine[:, None, None, None], queries[picked], jnp.zeros((), queries.dtype))
    incoming = lax.all_to_all(outgoing, "grp", 0, 0, tiled=True)

    my_slots = lax.dynamic_slice_in_dim(slot_request, group_idx * slot_count, slot_count)
    slot_queries = incoming[my_slots // requests]
    cache_keys = cache_kv[:, 0]
    cache_values = cache_kv[:, 1]
    slot_scores = (
        jnp.einsum("sakw,scw->sakc", slot_queries, cache_keys, preferred_element_type=jnp.float32)
        * score_scale
    )
    in_cache = (jnp.arange(cache_size, dtype=jnp.int32)[None, :] < cache_len[:, None])[
        :, None, None, :
    ]
    slot_peak, slot_den, slot_num = softmax_piece(
        slot_scores, in_cache, cache_values, "sakc,scw->sakw"
    )

    packed = jnp.concatenate([slot_num, slot_den[..., None], slot_peak[..., None]], axis=-1)
    to_home = (my_slots // requests)[None, :] == jnp.arange(group_count, dtype=jnp.int32)[:, None]
    returning = jnp.sum(
        jnp.where(to_home[:, :, None, None, None], packed[None], 0.0), axis=1
    )
    back = lax.all_to_all(returning, "grp", 0, 0, tiled=True)
    back_num = back[..., :head_width]
    back_den = back[..., head_width]
    back_peak = back[..., head_width + 1]

    home_ids = group_idx * requests + jnp.arange(requests, dtype=jnp.int32)
    matched = jnp.any(slot_table[None, :, :] == home_ids[:, None, None], axis=2)
    candidate = jnp.where(matched[:, :, None, None], back_peak[None], -jnp.inf)
    running_max = jnp.maximum(tree_peak, jnp.max(candidate, axis=1))
    rescale = jnp.exp(tree_peak - running_max)
    weight = jnp.exp(candidate - running_max[:, None])
    denominator = tree_den * rescale + jnp.sum(weight * back_den[None], axis=1)
    numerator = tree_num * rescale[..., None] + jnp.sum(
        weight[..., None] * back_num[None], axis=1
    )
    mixed = gate_probs[..., None] * numerator / denominator[..., None]
    return mixed.reshape(requests, kept_rows, topk_count, head_width).astype(jnp.bfloat16)


def solution(mesh):
    in_specs = (
        P("grp", None, "mdl"),
        P(None, None, "mdl"),
        P(None, None, "mdl"),
        P(),
        P("grp", None, None),
        P("grp", None, None),
        P("grp", None),
        P("grp", None, None, "mdl"),
        P("grp"),
        P(),
    )
    out_specs = P("grp", None, None, "mdl")
    return jax.shard_map(
        on_device, mesh=mesh, in_specs=in_specs, out_specs=out_specs, check_vma=False
    )
```

```python
import jax
import jax.numpy as jnp
from jax import lax
from jax.sharding import PartitionSpec as P

HEAD_SIZE = 128


def softmax_piece(scores, usable, values, contract):
    masked = jnp.where(usable, scores, -jnp.inf)
    peak_score = jnp.max(masked, axis=-1)
    weights_low = jnp.exp(masked - peak_score[..., None]).astype(jnp.bfloat16)
    denominator = jnp.sum(weights_low.astype(jnp.float32), axis=-1)
    numerator = jnp.einsum(contract, weights_low, values, preferred_element_type=jnp.float32)
    return (peak_score, denominator, numerator)


def on_device(
    draft_hidden,
    q_weight,
    kv_weight,
    router_weight,
    routes,
    tree_mask,
    accepted,
    cache_kv,
    cache_len,
    slot_request,
):
    highest = lax.Precision.HIGHEST
    requests, drafts, part_width = draft_hidden.shape
    experts = q_weight.shape[0]
    head_width = q_weight.shape[2]
    head_count = head_width // HEAD_SIZE
    topk_count = routes.shape[2]
    kept_rows = accepted.shape[1]
    score_scale = HEAD_SIZE ** (-0.5)
    group_count = lax.axis_size("grp")
    group_idx = lax.axis_index("grp")
    slot_count = cache_kv.shape[0]
    cache_size = cache_kv.shape[2]

    hidden = lax.all_gather(draft_hidden, "mdl", axis=2, tiled=True)
    acc_hidden = jnp.take_along_axis(hidden, accepted[:, :, None], axis=1)
    acc_routes = jnp.take_along_axis(routes, accepted[:, :, None], axis=1)
    acc_mask = jnp.take_along_axis(tree_mask, accepted[:, :, None], axis=1)

    q_sum = jnp.einsum("rad,edw->raew", acc_hidden, q_weight, preferred_element_type=jnp.float32)
    kv_sum = jnp.einsum("rtd,cdw->rtcw", hidden, kv_weight, preferred_element_type=jnp.float32)
    logit_sum = jnp.einsum(
        "rad,de->rae", acc_hidden.astype(jnp.float32), router_weight, precision=highest
    )
    chosen_mask = acc_routes[..., None] == jnp.arange(experts, dtype=jnp.int32)
    chosen = jnp.sum(jnp.where(chosen_mask, logit_sum[:, :, None, :], 0.0), axis=3)
    gate_probs = jax.nn.softmax(chosen, axis=-1)
    queries = jnp.sum(jnp.where(chosen_mask[..., None], q_sum[:, :, None], 0.0), axis=3)
    queries = queries.astype(jnp.bfloat16)
    draft_keys = kv_sum[:, :, 0].astype(jnp.bfloat16)
    draft_values = kv_sum[:, :, 1].astype(jnp.bfloat16)

    tree_scores = (
        jnp.einsum("rakw,rjw->rakj", queries, draft_keys, preferred_element_type=jnp.float32)
        * score_scale
    )
    tree_peak, tree_den, tree_num = softmax_piece(
        tree_scores, (acc_mask > 0)[:, :, None, :], draft_values, "rakj,rjw->rakw"
    )

    slot_table = slot_request.reshape(group_count, slot_count)
    home_of = slot_table // requests
    local_of = slot_table % requests
    mine = home_of == group_idx
    picked = jnp.sum(jnp.where(mine, local_of, 0), axis=1)
    any_mine = jnp.any(mine, axis=1)
    query_rows = queries.reshape(requests, kept_rows * topk_count, head_width)
    outgoing = jnp.where(
        any_mine[:, None, None],
        jnp.where((picked == 1)[:, None, None], query_rows[1][None], query_rows[0][None]),
        jnp.zeros((), query_rows.dtype),
    )
    incoming = lax.all_to_all(outgoing, "grp", 0, 0, tiled=True)

    my_slots = lax.dynamic_slice_in_dim(slot_request, group_idx * slot_count, slot_count)
    slot_queries = incoming[my_slots // requests].reshape(
        slot_count, kept_rows, topk_count, head_width
    )
    cache_keys = cache_kv[:, 0]
    cache_values = cache_kv[:, 1]
    slot_scores = (
        jnp.einsum("sakw,scw->sakc", slot_queries, cache_keys, preferred_element_type=jnp.float32)
        * score_scale
    )
    in_cache = (jnp.arange(cache_size, dtype=jnp.int32)[None, :] < cache_len[:, None])[
        :, None, None, :
    ]
    slot_peak, slot_den, slot_num = softmax_piece(
        slot_scores, in_cache, cache_values, "sakc,scw->sakw"
    )

    peak_low = lax.reduce_precision(slot_peak, exponent_bits=8, mantissa_bits=7)
    shift = jnp.exp(slot_peak - peak_low)
    shifted_num = slot_num * shift[..., None]
    shifted_den = slot_den * shift
    den_high = lax.reduce_precision(shifted_den, exponent_bits=8, mantissa_bits=7)
    den_rest = shifted_den - den_high
    row_count = kept_rows * topk_count
    facts = jnp.stack(
        [v.reshape(slot_count, row_count) for v in (peak_low, den_high, den_rest)], axis=1
    ).astype(jnp.bfloat16)
    facts = jnp.pad(facts, ((0, 0), (0, row_count - 3), (0, head_width - row_count)))
    packed = jnp.concatenate(
        [shifted_num.astype(jnp.bfloat16).reshape(slot_count, row_count, head_width), facts],
        axis=1,
    )
    to_home = (my_slots // requests)[None, :] == jnp.arange(group_count, dtype=jnp.int32)[:, None]
    returning = jnp.zeros((), packed.dtype)
    for i in range(slot_count):
        returning = jnp.where(to_home[:, i, None, None], packed[i][None], returning)
    back = lax.all_to_all(returning, "grp", 0, 0, tiled=True)
    back_num = back[:, :row_count].astype(jnp.float32).reshape(
        group_count, kept_rows, topk_count, head_width
    )
    back_facts = back[:, row_count:row_count + 3, :row_count].astype(jnp.float32)
    back_peak = back_facts[:, 0].reshape(group_count, kept_rows, topk_count)
    back_den = (back_facts[:, 1] + back_facts[:, 2]).reshape(group_count, kept_rows, topk_count)

    home_ids = group_idx * requests + jnp.arange(requests, dtype=jnp.int32)
    matched = jnp.any(slot_table[None, :, :] == home_ids[:, None, None], axis=2)
    candidate = jnp.where(matched[:, :, None, None], back_peak[None], -jnp.inf)
    running_max = jnp.maximum(tree_peak, jnp.max(candidate, axis=1))
    rescale = jnp.exp(tree_peak - running_max)
    weight = jnp.exp(candidate - running_max[:, None])
    denominator = tree_den * rescale + jnp.sum(weight * back_den[None], axis=1)
    numerator = tree_num * rescale[..., None] + jnp.sum(
        weight[..., None] * back_num[None], axis=1
    )
    mixed = gate_probs[..., None] * numerator / denominator[..., None]
    return mixed.reshape(requests, kept_rows, topk_count, head_width).astype(jnp.bfloat16)


def solution(mesh):
    in_specs = (
        P("grp", None, "mdl"),
        P(None, None, "mdl"),
        P(None, None, "mdl"),
        P(),
        P("grp", None, None),
        P("grp", None, None),
        P("grp", None),
        P("grp", None, None, "mdl"),
        P("grp"),
        P(),
    )
    out_specs = P("grp", None, None, "mdl")
    return jax.shard_map(
        on_device, mesh=mesh, in_specs=in_specs, out_specs=out_specs, check_vma=False
    )
```

```python
import jax
import jax.numpy as jnp
from jax import lax
from jax.sharding import PartitionSpec as P

HEAD_SIZE = 128


def softmax_piece(scores, usable, values, contract):
    masked = jnp.where(usable, scores, -jnp.inf)
    peak_score = jnp.max(masked, axis=-1)
    weights_low = jnp.exp(masked - peak_score[..., None]).astype(jnp.bfloat16)
    denominator = jnp.sum(weights_low.astype(jnp.float32), axis=-1)
    numerator = jnp.einsum(contract, weights_low, values, preferred_element_type=jnp.float32)
    return (peak_score, denominator, numerator)


def on_device(
    draft_hidden,
    q_weight,
    kv_weight,
    router_weight,
    routes,
    tree_mask,
    accepted,
    cache_kv,
    cache_len,
    slot_request,
):
    highest = lax.Precision.HIGHEST
    requests, drafts, part_width = draft_hidden.shape
    experts = q_weight.shape[0]
    head_width = q_weight.shape[2]
    head_count = head_width // HEAD_SIZE
    topk_count = routes.shape[2]
    kept_rows = accepted.shape[1]
    score_scale = HEAD_SIZE ** (-0.5)
    group_count = lax.axis_size("grp")
    group_idx = lax.axis_index("grp")
    slot_count = cache_kv.shape[0]
    cache_size = cache_kv.shape[2]

    model_count = lax.axis_size("mdl")
    hidden_parts = lax.all_to_all(
        jnp.broadcast_to(draft_hidden[None], (model_count,) + draft_hidden.shape),
        "mdl",
        0,
        0,
        tiled=True,
    )
    hidden = hidden_parts.transpose(1, 2, 0, 3).reshape(requests, drafts, model_count * part_width)
    acc_hidden = jnp.take_along_axis(hidden, accepted[:, :, None], axis=1)
    acc_routes = jnp.take_along_axis(routes, accepted[:, :, None], axis=1)
    acc_mask = jnp.take_along_axis(tree_mask, accepted[:, :, None], axis=1)

    q_sum = jnp.einsum("rad,edw->raew", acc_hidden, q_weight, preferred_element_type=jnp.float32)
    kv_sum = jnp.einsum("rtd,cdw->rtcw", hidden, kv_weight, preferred_element_type=jnp.float32)
    logit_sum = jnp.einsum(
        "rad,de->rae", acc_hidden.astype(jnp.float32), router_weight, precision=highest
    )
    chosen_mask = acc_routes[..., None] == jnp.arange(experts, dtype=jnp.int32)
    chosen = jnp.sum(jnp.where(chosen_mask, logit_sum[:, :, None, :], 0.0), axis=3)
    gate_probs = jax.nn.softmax(chosen, axis=-1)
    queries = jnp.sum(jnp.where(chosen_mask[..., None], q_sum[:, :, None], 0.0), axis=3)
    queries = queries.astype(jnp.bfloat16)
    draft_keys = kv_sum[:, :, 0].astype(jnp.bfloat16)
    draft_values = kv_sum[:, :, 1].astype(jnp.bfloat16)

    tree_scores = (
        jnp.einsum("rakw,rjw->rakj", queries, draft_keys, preferred_element_type=jnp.float32)
        * score_scale
    )
    tree_peak, tree_den, tree_num = softmax_piece(
        tree_scores, (acc_mask > 0)[:, :, None, :], draft_values, "rakj,rjw->rakw"
    )

    slot_table = slot_request.reshape(group_count, slot_count)
    home_of = slot_table // requests
    local_of = slot_table % requests
    mine = home_of == group_idx
    picked = jnp.sum(jnp.where(mine, local_of, 0), axis=1)
    any_mine = jnp.any(mine, axis=1)
    query_rows = queries.reshape(requests, kept_rows * topk_count, head_width)
    outgoing = jnp.where(
        any_mine[:, None, None],
        jnp.where((picked == 1)[:, None, None], query_rows[1][None], query_rows[0][None]),
        jnp.zeros((), query_rows.dtype),
    )
    incoming = lax.all_to_all(outgoing, "grp", 0, 0, tiled=True)

    my_slots = lax.dynamic_slice_in_dim(slot_request, group_idx * slot_count, slot_count)
    slot_queries = incoming[my_slots // requests].reshape(
        slot_count, kept_rows, topk_count, head_width
    )
    cache_keys = cache_kv[:, 0]
    cache_values = cache_kv[:, 1]
    slot_scores = (
        jnp.einsum("sakw,scw->sakc", slot_queries, cache_keys, preferred_element_type=jnp.float32)
        * score_scale
    )
    in_cache = (jnp.arange(cache_size, dtype=jnp.int32)[None, :] < cache_len[:, None])[
        :, None, None, :
    ]
    slot_peak, slot_den, slot_num = softmax_piece(
        slot_scores, in_cache, cache_values, "sakc,scw->sakw"
    )

    peak_low = lax.reduce_precision(slot_peak, exponent_bits=8, mantissa_bits=7)
    shift = jnp.exp(slot_peak - peak_low)
    shifted_num = slot_num * shift[..., None]
    shifted_den = slot_den * shift
    den_high = lax.reduce_precision(shifted_den, exponent_bits=8, mantissa_bits=7)
    den_rest = shifted_den - den_high
    row_count = kept_rows * topk_count
    facts = jnp.stack(
        [v.reshape(slot_count, row_count) for v in (peak_low, den_high, den_rest)], axis=1
    ).astype(jnp.bfloat16)
    facts = jnp.pad(facts, ((0, 0), (0, row_count - 3), (0, head_width - row_count)))
    packed = jnp.concatenate(
        [shifted_num.astype(jnp.bfloat16).reshape(slot_count, row_count, head_width), facts],
        axis=1,
    )
    to_home = (my_slots // requests)[None, :] == jnp.arange(group_count, dtype=jnp.int32)[:, None]
    returning = jnp.zeros((), packed.dtype)
    for i in range(slot_count):
        returning = jnp.where(to_home[:, i, None, None], packed[i][None], returning)
    back = lax.all_to_all(returning, "grp", 0, 0, tiled=True)
    back_num = back[:, :row_count].astype(jnp.float32).reshape(
        group_count, kept_rows, topk_count, head_width
    )
    back_facts = back[:, row_count:row_count + 3, :row_count].astype(jnp.float32)
    back_peak = back_facts[:, 0].reshape(group_count, kept_rows, topk_count)
    back_den = (back_facts[:, 1] + back_facts[:, 2]).reshape(group_count, kept_rows, topk_count)

    home_ids = group_idx * requests + jnp.arange(requests, dtype=jnp.int32)
    matched = jnp.any(slot_table[None, :, :] == home_ids[:, None, None], axis=2)
    candidate = jnp.where(matched[:, :, None, None], back_peak[None], -jnp.inf)
    running_max = jnp.maximum(tree_peak, jnp.max(candidate, axis=1))
    rescale = jnp.exp(tree_peak - running_max)
    weight = jnp.exp(candidate - running_max[:, None])
    denominator = tree_den * rescale + jnp.sum(weight * back_den[None], axis=1)
    numerator = tree_num * rescale[..., None] + jnp.sum(
        weight[..., None] * back_num[None], axis=1
    )
    mixed = gate_probs[..., None] * numerator / denominator[..., None]
    return mixed.reshape(requests, kept_rows, topk_count, head_width).astype(jnp.bfloat16)


def solution(mesh):
    in_specs = (
        P("grp", None, "mdl"),
        P(None, None, "mdl"),
        P(None, None, "mdl"),
        P(),
        P("grp", None, None),
        P("grp", None, None),
        P("grp", None),
        P("grp", None, None, "mdl"),
        P("grp"),
        P(),
    )
    out_specs = P("grp", None, None, "mdl")
    return jax.shard_map(
        on_device, mesh=mesh, in_specs=in_specs, out_specs=out_specs, check_vma=False
    )
```

```python
import jax
import jax.numpy as jnp
from jax import lax
from jax.sharding import PartitionSpec as P

HEAD_SIZE = 128


def softmax_piece(scores, usable, values, contract):
    masked = jnp.where(usable, scores, -jnp.inf)
    peak_score = jnp.max(masked, axis=-1)
    weights_low = jnp.exp(masked - peak_score[..., None]).astype(jnp.bfloat16)
    denominator = jnp.sum(weights_low.astype(jnp.float32), axis=-1)
    numerator = jnp.einsum(contract, weights_low, values, preferred_element_type=jnp.float32)
    return (peak_score, denominator, numerator)


def on_device(
    draft_hidden,
    q_weight,
    kv_weight,
    router_weight,
    routes,
    tree_mask,
    accepted,
    cache_kv,
    cache_len,
    slot_request,
):
    highest = lax.Precision.HIGHEST
    requests, drafts, part_width = draft_hidden.shape
    experts = q_weight.shape[0]
    head_width = q_weight.shape[2]
    head_count = head_width // HEAD_SIZE
    topk_count = routes.shape[2]
    kept_rows = accepted.shape[1]
    score_scale = HEAD_SIZE ** (-0.5)
    group_count = lax.axis_size("grp")
    group_idx = lax.axis_index("grp")
    slot_count = cache_kv.shape[0]
    cache_size = cache_kv.shape[2]

    model_count = lax.axis_size("mdl")
    hidden_parts = lax.all_to_all(
        jnp.broadcast_to(draft_hidden[None], (model_count,) + draft_hidden.shape),
        "mdl",
        0,
        0,
        tiled=True,
    )
    hidden = hidden_parts.transpose(1, 2, 0, 3).reshape(requests, drafts, model_count * part_width)
    acc_hidden = jnp.take_along_axis(hidden, accepted[:, :, None], axis=1)
    acc_routes = jnp.take_along_axis(routes, accepted[:, :, None], axis=1)
    acc_mask = jnp.take_along_axis(tree_mask, accepted[:, :, None], axis=1)

    q_sum = jnp.einsum("rad,edw->raew", acc_hidden, q_weight, preferred_element_type=jnp.float32)
    kv_sum = jnp.einsum("rtd,cdw->rtcw", hidden, kv_weight, preferred_element_type=jnp.float32)
    logit_sum = jnp.einsum(
        "rad,de->rae", acc_hidden.astype(jnp.float32), router_weight, precision=highest
    )
    chosen_mask = acc_routes[..., None] == jnp.arange(experts, dtype=jnp.int32)
    chosen = jnp.sum(jnp.where(chosen_mask, logit_sum[:, :, None, :], 0.0), axis=3)
    gate_probs = jax.nn.softmax(chosen, axis=-1)
    queries = jnp.sum(jnp.where(chosen_mask[..., None], q_sum[:, :, None], 0.0), axis=3)
    queries = queries.astype(jnp.bfloat16)
    draft_keys = kv_sum[:, :, 0].astype(jnp.bfloat16)
    draft_values = kv_sum[:, :, 1].astype(jnp.bfloat16)

    tree_scores = (
        jnp.einsum("rakw,rjw->rakj", queries, draft_keys, preferred_element_type=jnp.float32)
        * score_scale
    )
    tree_peak, tree_den, tree_num = softmax_piece(
        tree_scores, (acc_mask > 0)[:, :, None, :], draft_values, "rakj,rjw->rakw"
    )

    slot_table = slot_request.reshape(group_count, slot_count)
    home_of = slot_table // requests
    local_of = slot_table % requests
    mine = home_of == group_idx
    picked = jnp.sum(jnp.where(mine, local_of, 0), axis=1)
    any_mine = jnp.any(mine, axis=1)
    query_rows = queries.reshape(requests, kept_rows * topk_count * head_width)
    send_pick = (
        any_mine[:, None] & (picked[:, None] == jnp.arange(requests, dtype=jnp.int32)[None, :])
    ).astype(query_rows.dtype)
    outgoing = jnp.einsum(
        "dr,rx->dx", send_pick, query_rows, preferred_element_type=jnp.float32
    ).astype(query_rows.dtype)
    incoming = lax.all_to_all(
        outgoing.reshape(group_count, kept_rows * topk_count, head_width), "grp", 0, 0, tiled=True
    )

    my_slots = lax.dynamic_slice_in_dim(slot_request, group_idx * slot_count, slot_count)
    take_pick = (
        (my_slots // requests)[:, None] == jnp.arange(group_count, dtype=jnp.int32)[None, :]
    ).astype(incoming.dtype)
    slot_queries = (
        jnp.einsum(
            "sd,dx->sx",
            take_pick,
            incoming.reshape(group_count, -1),
            preferred_element_type=jnp.float32,
        )
        .astype(incoming.dtype)
        .reshape(slot_count, kept_rows, topk_count, head_width)
    )
    cache_keys = cache_kv[:, 0]
    cache_values = cache_kv[:, 1]
    slot_scores = (
        jnp.einsum("sakw,scw->sakc", slot_queries, cache_keys, preferred_element_type=jnp.float32)
        * score_scale
    )
    in_cache = (jnp.arange(cache_size, dtype=jnp.int32)[None, :] < cache_len[:, None])[
        :, None, None, :
    ]
    slot_peak, slot_den, slot_num = softmax_piece(
        slot_scores, in_cache, cache_values, "sakc,scw->sakw"
    )

    peak_low = lax.reduce_precision(slot_peak, exponent_bits=8, mantissa_bits=7)
    shift = jnp.exp(slot_peak - peak_low)
    shifted_num = slot_num * shift[..., None]
    shifted_den = slot_den * shift
    den_high = lax.reduce_precision(shifted_den, exponent_bits=8, mantissa_bits=7)
    den_rest = shifted_den - den_high
    row_count = kept_rows * topk_count
    facts = jnp.stack(
        [v.reshape(slot_count, row_count) for v in (peak_low, den_high, den_rest)], axis=1
    ).astype(jnp.bfloat16)
    facts = jnp.pad(facts, ((0, 0), (0, row_count - 3), (0, head_width - row_count)))
    packed = jnp.concatenate(
        [shifted_num.astype(jnp.bfloat16).reshape(slot_count, row_count, head_width), facts],
        axis=1,
    )
    returning = (
        jnp.einsum(
            "ds,sx->dx",
            take_pick.T,
            packed.reshape(slot_count, -1),
            preferred_element_type=jnp.float32,
        )
        .astype(packed.dtype)
        .reshape(group_count, 2 * row_count, head_width)
    )
    back = lax.all_to_all(returning, "grp", 0, 0, tiled=True)
    back_num = back[:, :row_count].astype(jnp.float32).reshape(
        group_count, kept_rows, topk_count, head_width
    )
    back_facts = back[:, row_count:row_count + 3, :row_count].astype(jnp.float32)
    back_peak = back_facts[:, 0].reshape(group_count, kept_rows, topk_count)
    back_den = (back_facts[:, 1] + back_facts[:, 2]).reshape(group_count, kept_rows, topk_count)

    home_ids = group_idx * requests + jnp.arange(requests, dtype=jnp.int32)
    matched = jnp.any(slot_table[None, :, :] == home_ids[:, None, None], axis=2)
    candidate = jnp.where(matched[:, :, None, None], back_peak[None], -jnp.inf)
    running_max = jnp.maximum(tree_peak, jnp.max(candidate, axis=1))
    rescale = jnp.exp(tree_peak - running_max)
    weight = jnp.exp(candidate - running_max[:, None])
    denominator = tree_den * rescale + jnp.sum(weight * back_den[None], axis=1)
    numerator = tree_num * rescale[..., None] + jnp.sum(
        weight[..., None] * back_num[None], axis=1
    )
    mixed = gate_probs[..., None] * numerator / denominator[..., None]
    return mixed.reshape(requests, kept_rows, topk_count, head_width).astype(jnp.bfloat16)


def solution(mesh):
    in_specs = (
        P("grp", None, "mdl"),
        P(None, None, "mdl"),
        P(None, None, "mdl"),
        P(),
        P("grp", None, None),
        P("grp", None, None),
        P("grp", None),
        P("grp", None, None, "mdl"),
        P("grp"),
        P(),
    )
    out_specs = P("grp", None, None, "mdl")
    return jax.shard_map(
        on_device, mesh=mesh, in_specs=in_specs, out_specs=out_specs, check_vma=False
    )
```

```python
import jax
import jax.numpy as jnp
import functools

from jax import lax
from jax.experimental import pallas as pl
from jax.experimental.pallas import tpu as pltpu
from jax.sharding import PartitionSpec as P

HEAD_SIZE = 128


def softmax_piece(scores, usable, values, contract):
    masked = jnp.where(usable, scores, -jnp.inf)
    peak_score = jnp.max(masked, axis=-1)
    weights_low = jnp.exp(masked - peak_score[..., None]).astype(jnp.bfloat16)
    denominator = jnp.sum(weights_low.astype(jnp.float32), axis=-1)
    numerator = jnp.einsum(contract, weights_low, values, preferred_element_type=jnp.float32)
    return (peak_score, denominator, numerator)


def slot_attention_kernel(home_ref, len_ref, incoming_ref, cache_ref, out_ref, *, scale):
    slot_count = cache_ref.shape[0]
    rows = incoming_ref.shape[1]
    out_ref[...] = jnp.zeros(out_ref.shape, out_ref.dtype)
    for i in range(slot_count):
        home = home_ref[i]
        scores = (
            lax.dot_general(
                incoming_ref[home],
                cache_ref[i, 0],
                (((1,), (1,)), ((), ())),
                preferred_element_type=jnp.float32,
            )
            * scale
        )
        position = lax.broadcasted_iota(jnp.int32, scores.shape, 1)
        masked = jnp.where(position < len_ref[i], scores, -jnp.inf)
        peak = jnp.max(masked, axis=1, keepdims=True)
        weights = jnp.exp(masked - peak).astype(jnp.bfloat16)
        den = jnp.sum(weights.astype(jnp.float32), axis=1, keepdims=True)
        num = jnp.dot(weights, cache_ref[i, 1], preferred_element_type=jnp.float32)
        peak_low = peak.astype(jnp.bfloat16).astype(jnp.float32)
        shift = jnp.exp(peak - peak_low)
        shifted_den = den * shift
        den_high = shifted_den.astype(jnp.bfloat16).astype(jnp.float32)
        den_rest = shifted_den - den_high
        lane = lax.broadcasted_iota(jnp.int32, (rows, out_ref.shape[2]), 1)
        facts = jnp.where(
            lane == 0,
            peak_low,
            jnp.where(lane == 1, den_high, jnp.where(lane == 2, den_rest, 0.0)),
        )
        out_ref[home, :rows, :] = (num * shift).astype(out_ref.dtype)
        out_ref[home, rows:, :] = facts.astype(out_ref.dtype)


def slot_attention(home, cache_len, incoming, cache_kv, scale):
    groups, rows, width = incoming.shape
    slot_count, _, cache_size, _ = cache_kv.shape
    flops = 4 * slot_count * rows * cache_size * width
    moved = 2 * (cache_kv.size + incoming.size + 2 * groups * rows * width)
    return pl.pallas_call(
        functools.partial(slot_attention_kernel, scale=scale),
        out_shape=jax.ShapeDtypeStruct((groups, 2 * rows, width), incoming.dtype),
        in_specs=[
            pl.BlockSpec(memory_space=pltpu.SMEM),
            pl.BlockSpec(memory_space=pltpu.SMEM),
            pl.BlockSpec(memory_space=pltpu.VMEM),
            pl.BlockSpec(memory_space=pltpu.VMEM),
        ],
        out_specs=pl.BlockSpec(memory_space=pltpu.VMEM),
        cost_estimate=pl.CostEstimate(
            flops=flops, transcendentals=slot_count * rows * cache_size, bytes_accessed=moved
        ),
    )(home, cache_len, incoming, cache_kv)


def on_device(
    draft_hidden,
    q_weight,
    kv_weight,
    router_weight,
    routes,
    tree_mask,
    accepted,
    cache_kv,
    cache_len,
    slot_request,
):
    highest = lax.Precision.HIGHEST
    requests, drafts, part_width = draft_hidden.shape
    experts = q_weight.shape[0]
    head_width = q_weight.shape[2]
    head_count = head_width // HEAD_SIZE
    topk_count = routes.shape[2]
    kept_rows = accepted.shape[1]
    score_scale = HEAD_SIZE ** (-0.5)
    group_count = lax.axis_size("grp")
    group_idx = lax.axis_index("grp")
    slot_count = cache_kv.shape[0]
    cache_size = cache_kv.shape[2]

    model_count = lax.axis_size("mdl")
    hidden_parts = lax.all_to_all(
        jnp.broadcast_to(draft_hidden[None], (model_count,) + draft_hidden.shape),
        "mdl",
        0,
        0,
        tiled=True,
    )
    hidden = hidden_parts.transpose(1, 2, 0, 3).reshape(requests, drafts, model_count * part_width)
    acc_hidden = jnp.take_along_axis(hidden, accepted[:, :, None], axis=1)
    acc_routes = jnp.take_along_axis(routes, accepted[:, :, None], axis=1)
    acc_mask = jnp.take_along_axis(tree_mask, accepted[:, :, None], axis=1)

    q_sum = jnp.einsum("rad,edw->raew", acc_hidden, q_weight, preferred_element_type=jnp.float32)
    kv_sum = jnp.einsum("rtd,cdw->rtcw", hidden, kv_weight, preferred_element_type=jnp.float32)
    logit_sum = jnp.einsum(
        "rad,de->rae", acc_hidden.astype(jnp.float32), router_weight, precision=highest
    )
    chosen_mask = acc_routes[..., None] == jnp.arange(experts, dtype=jnp.int32)
    chosen = jnp.sum(jnp.where(chosen_mask, logit_sum[:, :, None, :], 0.0), axis=3)
    gate_probs = jax.nn.softmax(chosen, axis=-1)
    queries = jnp.sum(jnp.where(chosen_mask[..., None], q_sum[:, :, None], 0.0), axis=3)
    queries = queries.astype(jnp.bfloat16)
    draft_keys = kv_sum[:, :, 0].astype(jnp.bfloat16)
    draft_values = kv_sum[:, :, 1].astype(jnp.bfloat16)

    tree_scores = (
        jnp.einsum("rakw,rjw->rakj", queries, draft_keys, preferred_element_type=jnp.float32)
        * score_scale
    )
    tree_peak, tree_den, tree_num = softmax_piece(
        tree_scores, (acc_mask > 0)[:, :, None, :], draft_values, "rakj,rjw->rakw"
    )

    slot_table = slot_request.reshape(group_count, slot_count)
    home_of = slot_table // requests
    local_of = slot_table % requests
    mine = home_of == group_idx
    picked = jnp.sum(jnp.where(mine, local_of, 0), axis=1)
    any_mine = jnp.any(mine, axis=1)
    query_rows = queries.reshape(requests, kept_rows * topk_count * head_width)
    send_pick = (
        any_mine[:, None] & (picked[:, None] == jnp.arange(requests, dtype=jnp.int32)[None, :])
    ).astype(query_rows.dtype)
    outgoing = jnp.einsum(
        "dr,rx->dx", send_pick, query_rows, preferred_element_type=jnp.float32
    ).astype(query_rows.dtype)
    incoming = lax.all_to_all(
        outgoing.reshape(group_count, kept_rows * topk_count, head_width), "grp", 0, 0, tiled=True
    )

    my_slots = lax.dynamic_slice_in_dim(slot_request, group_idx * slot_count, slot_count)
    row_count = kept_rows * topk_count
    returning = slot_attention(my_slots // requests, cache_len, incoming, cache_kv, score_scale)
    back = lax.all_to_all(returning, "grp", 0, 0, tiled=True)
    back_num = back[:, :row_count].astype(jnp.float32).reshape(
        group_count, kept_rows, topk_count, head_width
    )
    back_facts = back[:, row_count:, :3].astype(jnp.float32)
    back_peak = back_facts[..., 0].reshape(group_count, kept_rows, topk_count)
    back_den = (back_facts[..., 1] + back_facts[..., 2]).reshape(group_count, kept_rows, topk_count)

    home_ids = group_idx * requests + jnp.arange(requests, dtype=jnp.int32)
    matched = jnp.any(slot_table[None, :, :] == home_ids[:, None, None], axis=2)
    candidate = jnp.where(matched[:, :, None, None], back_peak[None], -jnp.inf)
    running_max = jnp.maximum(tree_peak, jnp.max(candidate, axis=1))
    rescale = jnp.exp(tree_peak - running_max)
    weight = jnp.exp(candidate - running_max[:, None])
    denominator = tree_den * rescale + jnp.sum(weight * back_den[None], axis=1)
    numerator = tree_num * rescale[..., None] + jnp.sum(
        weight[..., None] * back_num[None], axis=1
    )
    mixed = gate_probs[..., None] * numerator / denominator[..., None]
    return mixed.reshape(requests, kept_rows, topk_count, head_width).astype(jnp.bfloat16)


def solution(mesh):
    in_specs = (
        P("grp", None, "mdl"),
        P(None, None, "mdl"),
        P(None, None, "mdl"),
        P(),
        P("grp", None, None),
        P("grp", None, None),
        P("grp", None),
        P("grp", None, None, "mdl"),
        P("grp"),
        P(),
    )
    out_specs = P("grp", None, None, "mdl")
    return jax.shard_map(
        on_device, mesh=mesh, in_specs=in_specs, out_specs=out_specs, check_vma=False
    )
```

```python
import jax
import jax.numpy as jnp
import functools

from jax import lax
from jax.experimental import pallas as pl
from jax.experimental.pallas import tpu as pltpu
from jax.sharding import PartitionSpec as P

HEAD_SIZE = 128


def softmax_piece(scores, usable, values, contract):
    masked = jnp.where(usable, scores, -jnp.inf)
    peak_score = jnp.max(masked, axis=-1)
    weights_low = jnp.exp(masked - peak_score[..., None]).astype(jnp.bfloat16)
    denominator = jnp.sum(weights_low.astype(jnp.float32), axis=-1)
    numerator = jnp.einsum(contract, weights_low, values, preferred_element_type=jnp.float32)
    return (peak_score, denominator, numerator)


def slot_attention_kernel(home_ref, len_ref, incoming_ref, cache_ref, out_ref, *, scale):
    slot_count = cache_ref.shape[0]
    rows = incoming_ref.shape[1]
    out_ref[...] = jnp.zeros(out_ref.shape, out_ref.dtype)
    for i in range(slot_count):
        home = home_ref[i]
        scores = (
            lax.dot_general(
                incoming_ref[home],
                cache_ref[i, 0],
                (((1,), (1,)), ((), ())),
                preferred_element_type=jnp.float32,
            )
            * scale
        )
        position = lax.broadcasted_iota(jnp.int32, scores.shape, 1)
        masked = jnp.where(position < len_ref[i], scores, -jnp.inf)
        peak = jnp.max(masked, axis=1, keepdims=True)
        weights = jnp.exp(masked - peak).astype(jnp.bfloat16)
        den = jnp.sum(weights.astype(jnp.float32), axis=1, keepdims=True)
        num = jnp.dot(weights, cache_ref[i, 1], preferred_element_type=jnp.float32)
        peak_low = peak.astype(jnp.bfloat16).astype(jnp.float32)
        shift = jnp.exp(peak - peak_low)
        shifted_den = den * shift
        den_high = shifted_den.astype(jnp.bfloat16).astype(jnp.float32)
        den_rest = shifted_den - den_high
        lane = lax.broadcasted_iota(jnp.int32, (rows, out_ref.shape[2]), 1)
        facts = jnp.where(
            lane == 0,
            peak_low,
            jnp.where(lane == 1, den_high, jnp.where(lane == 2, den_rest, 0.0)),
        )
        out_ref[home, :rows, :] = (num * shift).astype(out_ref.dtype)
        out_ref[home, rows:, :] = facts.astype(out_ref.dtype)


def slot_attention(home, cache_len, incoming, cache_kv, scale):
    groups, rows, width = incoming.shape
    slot_count, _, cache_size, _ = cache_kv.shape
    flops = 4 * slot_count * rows * cache_size * width
    moved = 2 * (cache_kv.size + incoming.size + 2 * groups * rows * width)
    return pl.pallas_call(
        functools.partial(slot_attention_kernel, scale=scale),
        out_shape=jax.ShapeDtypeStruct((groups, 2 * rows, width), incoming.dtype),
        in_specs=[
            pl.BlockSpec(memory_space=pltpu.SMEM),
            pl.BlockSpec(memory_space=pltpu.SMEM),
            pl.BlockSpec(memory_space=pltpu.VMEM),
            pl.BlockSpec(memory_space=pltpu.VMEM),
        ],
        out_specs=pl.BlockSpec(memory_space=pltpu.VMEM),
        cost_estimate=pl.CostEstimate(
            flops=flops, transcendentals=slot_count * rows * cache_size, bytes_accessed=moved
        ),
    )(home, cache_len, incoming, cache_kv)


def on_device(
    draft_hidden,
    q_weight,
    kv_weight,
    router_weight,
    routes,
    tree_mask,
    accepted,
    cache_kv,
    cache_len,
    slot_request,
):
    highest = lax.Precision.HIGHEST
    requests, drafts, part_width = draft_hidden.shape
    experts = q_weight.shape[0]
    head_width = q_weight.shape[2]
    head_count = head_width // HEAD_SIZE
    topk_count = routes.shape[2]
    kept_rows = accepted.shape[1]
    score_scale = HEAD_SIZE ** (-0.5)
    group_count = lax.axis_size("grp")
    group_idx = lax.axis_index("grp")
    slot_count = cache_kv.shape[0]
    cache_size = cache_kv.shape[2]

    model_count = lax.axis_size("mdl")
    hidden_parts = lax.all_to_all(
        jnp.broadcast_to(draft_hidden[None], (model_count,) + draft_hidden.shape),
        "mdl",
        0,
        0,
        tiled=True,
    )
    hidden = hidden_parts.transpose(1, 2, 0, 3).reshape(requests, drafts, model_count * part_width)
    row_pick = accepted[:, :, None] == jnp.arange(drafts, dtype=jnp.int32)[None, None, :]
    acc_hidden = jnp.einsum(
        "rat,rtd->rad", row_pick.astype(hidden.dtype), hidden, preferred_element_type=jnp.float32
    ).astype(hidden.dtype)
    acc_routes = jnp.sum(jnp.where(row_pick[..., None], routes[:, None], 0), axis=2)
    acc_mask = jnp.sum(jnp.where(row_pick[..., None], tree_mask[:, None], 0), axis=2)

    q_sum = jnp.einsum("rad,edw->raew", acc_hidden, q_weight, preferred_element_type=jnp.float32)
    kv_sum = jnp.einsum("rtd,cdw->rtcw", hidden, kv_weight, preferred_element_type=jnp.float32)
    logit_sum = jnp.einsum(
        "rad,de->rae", acc_hidden.astype(jnp.float32), router_weight, precision=highest
    )
    chosen_mask = acc_routes[..., None] == jnp.arange(experts, dtype=jnp.int32)
    chosen = jnp.sum(jnp.where(chosen_mask, logit_sum[:, :, None, :], 0.0), axis=3)
    gate_probs = jax.nn.softmax(chosen, axis=-1)
    queries = jnp.sum(jnp.where(chosen_mask[..., None], q_sum[:, :, None], 0.0), axis=3)
    queries = queries.astype(jnp.bfloat16)
    draft_keys = kv_sum[:, :, 0].astype(jnp.bfloat16)
    draft_values = kv_sum[:, :, 1].astype(jnp.bfloat16)

    tree_scores = (
        jnp.einsum("rakw,rjw->rakj", queries, draft_keys, preferred_element_type=jnp.float32)
        * score_scale
    )
    tree_peak, tree_den, tree_num = softmax_piece(
        tree_scores, (acc_mask > 0)[:, :, None, :], draft_values, "rakj,rjw->rakw"
    )

    slot_table = slot_request.reshape(group_count, slot_count)
    home_of = slot_table // requests
    local_of = slot_table % requests
    mine = home_of == group_idx
    picked = jnp.sum(jnp.where(mine, local_of, 0), axis=1)
    any_mine = jnp.any(mine, axis=1)
    query_rows = queries.reshape(requests, kept_rows * topk_count, head_width)
    send_pick = (
        any_mine[:, None] & (picked[:, None] == jnp.arange(requests, dtype=jnp.int32)[None, :])
    ).astype(query_rows.dtype)
    outgoing = jnp.einsum(
        "dr,rxw->dxw", send_pick, query_rows, preferred_element_type=jnp.float32
    ).astype(query_rows.dtype)
    incoming = lax.all_to_all(outgoing, "grp", 0, 0, tiled=True)

    my_slots = lax.dynamic_slice_in_dim(slot_request, group_idx * slot_count, slot_count)
    row_count = kept_rows * topk_count
    returning = slot_attention(my_slots // requests, cache_len, incoming, cache_kv, score_scale)
    back = lax.all_to_all(returning, "grp", 0, 0, tiled=True)
    back_num = back[:, :row_count].astype(jnp.float32).reshape(
        group_count, kept_rows, topk_count, head_width
    )
    back_facts = back[:, row_count:, :3].astype(jnp.float32)
    back_peak = back_facts[..., 0].reshape(group_count, kept_rows, topk_count)
    back_den = (back_facts[..., 1] + back_facts[..., 2]).reshape(group_count, kept_rows, topk_count)

    home_ids = group_idx * requests + jnp.arange(requests, dtype=jnp.int32)
    matched = jnp.any(slot_table[None, :, :] == home_ids[:, None, None], axis=2)
    candidate = jnp.where(matched[:, :, None, None], back_peak[None], -jnp.inf)
    running_max = jnp.maximum(tree_peak, jnp.max(candidate, axis=1))
    rescale = jnp.exp(tree_peak - running_max)
    weight = jnp.exp(candidate - running_max[:, None])
    denominator = tree_den * rescale + jnp.sum(weight * back_den[None], axis=1)
    numerator = tree_num * rescale[..., None] + jnp.sum(
        weight[..., None] * back_num[None], axis=1
    )
    mixed = gate_probs[..., None] * numerator / denominator[..., None]
    return mixed.reshape(requests, kept_rows, topk_count, head_width).astype(jnp.bfloat16)


def solution(mesh):
    in_specs = (
        P("grp", None, "mdl"),
        P(None, None, "mdl"),
        P(None, None, "mdl"),
        P(),
        P("grp", None, None),
        P("grp", None, None),
        P("grp", None),
        P("grp", None, None, "mdl"),
        P("grp"),
        P(),
    )
    out_specs = P("grp", None, None, "mdl")
    return jax.shard_map(
        on_device, mesh=mesh, in_specs=in_specs, out_specs=out_specs, check_vma=False
    )
```

```python
import jax
import jax.numpy as jnp
import functools

from jax import lax
from jax.experimental import pallas as pl
from jax.experimental.pallas import tpu as pltpu
from jax.sharding import PartitionSpec as P

HEAD_SIZE = 128


def softmax_piece(scores, usable, values, contract):
    masked = jnp.where(usable, scores, -jnp.inf)
    peak_score = jnp.max(masked, axis=-1)
    weights_low = jnp.exp(masked - peak_score[..., None]).astype(jnp.bfloat16)
    denominator = jnp.sum(weights_low.astype(jnp.float32), axis=-1)
    numerator = jnp.einsum(contract, weights_low, values, preferred_element_type=jnp.float32)
    return (peak_score, denominator, numerator)


def slot_attention_kernel(home_ref, len_ref, incoming_ref, cache_ref, out_ref, *, scale):
    slot_count = cache_ref.shape[0]
    rows = incoming_ref.shape[1]
    out_ref[...] = jnp.zeros(out_ref.shape, out_ref.dtype)
    for i in range(slot_count):
        home = home_ref[i]
        scores = (
            lax.dot_general(
                incoming_ref[home],
                cache_ref[i, 0],
                (((1,), (1,)), ((), ())),
                preferred_element_type=jnp.float32,
            )
            * scale
        )
        position = lax.broadcasted_iota(jnp.int32, scores.shape, 1)
        masked = jnp.where(position < len_ref[i], scores, -jnp.inf)
        peak = jnp.max(masked, axis=1, keepdims=True)
        weights = jnp.exp(masked - peak).astype(jnp.bfloat16)
        den = jnp.sum(weights.astype(jnp.float32), axis=1, keepdims=True)
        num = jnp.dot(weights, cache_ref[i, 1], preferred_element_type=jnp.float32)
        peak_low = peak.astype(jnp.bfloat16).astype(jnp.float32)
        shift = jnp.exp(peak - peak_low)
        shifted_den = den * shift
        den_high = shifted_den.astype(jnp.bfloat16).astype(jnp.float32)
        den_rest = shifted_den - den_high
        lane = lax.broadcasted_iota(jnp.int32, (rows, out_ref.shape[2]), 1)
        facts = jnp.where(
            lane == 0,
            peak_low,
            jnp.where(lane == 1, den_high, jnp.where(lane == 2, den_rest, 0.0)),
        )
        out_ref[home, :rows, :] = (num * shift).astype(out_ref.dtype)
        out_ref[home, rows:, :] = facts.astype(out_ref.dtype)


def slot_attention(home, cache_len, incoming, cache_kv, scale):
    groups, rows, width = incoming.shape
    slot_count, _, cache_size, _ = cache_kv.shape
    flops = 4 * slot_count * rows * cache_size * width
    moved = 2 * (cache_kv.size + incoming.size + 2 * groups * rows * width)
    return pl.pallas_call(
        functools.partial(slot_attention_kernel, scale=scale),
        out_shape=jax.ShapeDtypeStruct((groups, 2 * rows, width), incoming.dtype),
        in_specs=[
            pl.BlockSpec(memory_space=pltpu.SMEM),
            pl.BlockSpec(memory_space=pltpu.SMEM),
            pl.BlockSpec(memory_space=pltpu.VMEM),
            pl.BlockSpec(memory_space=pltpu.VMEM),
        ],
        out_specs=pl.BlockSpec(memory_space=pltpu.VMEM),
        cost_estimate=pl.CostEstimate(
            flops=flops, transcendentals=slot_count * rows * cache_size, bytes_accessed=moved
        ),
    )(home, cache_len, incoming, cache_kv)


def on_device(
    draft_hidden,
    q_weight,
    kv_weight,
    router_weight,
    routes,
    tree_mask,
    accepted,
    cache_kv,
    cache_len,
    slot_request,
):
    highest = lax.Precision.HIGHEST
    requests, drafts, part_width = draft_hidden.shape
    experts = q_weight.shape[0]
    head_width = q_weight.shape[2]
    head_count = head_width // HEAD_SIZE
    topk_count = routes.shape[2]
    kept_rows = accepted.shape[1]
    score_scale = HEAD_SIZE ** (-0.5)
    group_count = lax.axis_size("grp")
    group_idx = lax.axis_index("grp")
    slot_count = cache_kv.shape[0]
    cache_size = cache_kv.shape[2]

    row_pick = accepted[:, :, None] == jnp.arange(drafts, dtype=jnp.int32)[None, None, :]
    acc_part = jnp.einsum(
        "rat,rtd->rad",
        row_pick.astype(draft_hidden.dtype),
        draft_hidden,
        preferred_element_type=jnp.float32,
    ).astype(draft_hidden.dtype)
    acc_routes = jnp.sum(jnp.where(row_pick[..., None], routes[:, None], 0), axis=2)
    mask_rows = jnp.sum(jnp.where(row_pick[..., None], tree_mask[:, None], 0), axis=2)
    acc_mask = jnp.sum(jnp.where(row_pick[:, None, :, :], mask_rows[:, :, None, :], 0), axis=3)
    order = jnp.arange(kept_rows, dtype=jnp.int32)
    repeated = jnp.any(
        (accepted[:, :, None] == accepted[:, None, :]) & (order[None, None, :] < order[None, :, None]),
        axis=2,
    )
    usable_keys = (acc_mask > 0) & ~repeated[:, None, :]

    model_count = lax.axis_size("mdl")
    hidden_parts = lax.all_to_all(
        jnp.broadcast_to(acc_part[None], (model_count,) + acc_part.shape),
        "mdl",
        0,
        0,
        tiled=True,
    )
    acc_hidden = hidden_parts.transpose(1, 2, 0, 3).reshape(
        requests, kept_rows, model_count * part_width
    )

    q_sum = jnp.einsum("rad,edw->raew", acc_hidden, q_weight, preferred_element_type=jnp.float32)
    kv_sum = jnp.einsum("rtd,cdw->rtcw", acc_hidden, kv_weight, preferred_element_type=jnp.float32)
    logit_sum = jnp.einsum(
        "rad,de->rae", acc_hidden.astype(jnp.float32), router_weight, precision=highest
    )
    chosen_mask = acc_routes[..., None] == jnp.arange(experts, dtype=jnp.int32)
    chosen = jnp.sum(jnp.where(chosen_mask, logit_sum[:, :, None, :], 0.0), axis=3)
    gate_probs = jax.nn.softmax(chosen, axis=-1)
    queries = jnp.sum(jnp.where(chosen_mask[..., None], q_sum[:, :, None], 0.0), axis=3)
    queries = queries.astype(jnp.bfloat16)
    draft_keys = kv_sum[:, :, 0].astype(jnp.bfloat16)
    draft_values = kv_sum[:, :, 1].astype(jnp.bfloat16)

    tree_scores = (
        jnp.einsum("rakw,rjw->rakj", queries, draft_keys, preferred_element_type=jnp.float32)
        * score_scale
    )
    tree_peak, tree_den, tree_num = softmax_piece(
        tree_scores, usable_keys[:, :, None, :], draft_values, "rakj,rjw->rakw"
    )

    slot_table = slot_request.reshape(group_count, slot_count)
    home_of = slot_table // requests
    local_of = slot_table % requests
    mine = home_of == group_idx
    picked = jnp.sum(jnp.where(mine, local_of, 0), axis=1)
    any_mine = jnp.any(mine, axis=1)
    query_rows = queries.reshape(requests, kept_rows * topk_count, head_width)
    send_pick = (
        any_mine[:, None] & (picked[:, None] == jnp.arange(requests, dtype=jnp.int32)[None, :])
    ).astype(query_rows.dtype)
    outgoing = jnp.einsum(
        "dr,rxw->dxw", send_pick, query_rows, preferred_element_type=jnp.float32
    ).astype(query_rows.dtype)
    incoming = lax.all_to_all(outgoing, "grp", 0, 0, tiled=True)

    my_slots = lax.dynamic_slice_in_dim(slot_request, group_idx * slot_count, slot_count)
    row_count = kept_rows * topk_count
    returning = slot_attention(my_slots // requests, cache_len, incoming, cache_kv, score_scale)
    back = lax.all_to_all(returning, "grp", 0, 0, tiled=True)
    back_num = back[:, :row_count].astype(jnp.float32).reshape(
        group_count, kept_rows, topk_count, head_width
    )
    back_facts = back[:, row_count:, :3].astype(jnp.float32)
    back_peak = back_facts[..., 0].reshape(group_count, kept_rows, topk_count)
    back_den = (back_facts[..., 1] + back_facts[..., 2]).reshape(group_count, kept_rows, topk_count)

    home_ids = group_idx * requests + jnp.arange(requests, dtype=jnp.int32)
    matched = jnp.any(slot_table[None, :, :] == home_ids[:, None, None], axis=2)
    candidate = jnp.where(matched[:, :, None, None], back_peak[None], -jnp.inf)
    running_max = jnp.maximum(tree_peak, jnp.max(candidate, axis=1))
    rescale = jnp.exp(tree_peak - running_max)
    weight = jnp.exp(candidate - running_max[:, None])
    denominator = tree_den * rescale + jnp.sum(weight * back_den[None], axis=1)
    numerator = tree_num * rescale[..., None] + jnp.sum(
        weight[..., None] * back_num[None], axis=1
    )
    mixed = gate_probs[..., None] * numerator / denominator[..., None]
    return mixed.reshape(requests, kept_rows, topk_count, head_width).astype(jnp.bfloat16)


def solution(mesh):
    in_specs = (
        P("grp", None, "mdl"),
        P(None, None, "mdl"),
        P(None, None, "mdl"),
        P(),
        P("grp", None, None),
        P("grp", None, None),
        P("grp", None),
        P("grp", None, None, "mdl"),
        P("grp"),
        P(),
    )
    out_specs = P("grp", None, None, "mdl")
    return jax.shard_map(
        on_device, mesh=mesh, in_specs=in_specs, out_specs=out_specs, check_vma=False
    )
```

```python
import jax
import jax.numpy as jnp
import functools

from jax import lax
from jax.experimental import pallas as pl
from jax.experimental.pallas import tpu as pltpu
from jax.sharding import PartitionSpec as P

HEAD_SIZE = 128


def softmax_piece(scores, usable, values, contract):
    masked = jnp.where(usable, scores, -jnp.inf)
    peak_score = jnp.max(masked, axis=-1)
    weights_low = jnp.exp(masked - peak_score[..., None]).astype(jnp.bfloat16)
    denominator = jnp.sum(weights_low.astype(jnp.float32), axis=-1)
    numerator = jnp.einsum(contract, weights_low, values, preferred_element_type=jnp.float32)
    return (peak_score, denominator, numerator)


def slot_attention_kernel(
    home_ref, len_ref, incoming_ref, cache_hbm, out_ref, cache_buf, sems, *, scale
):
    slot_count = cache_buf.shape[0]
    rows = incoming_ref.shape[1]
    copies = [
        pltpu.make_async_copy(cache_hbm.at[i], cache_buf.at[i], sems.at[i])
        for i in range(slot_count)
    ]
    for copy in copies:
        copy.start()
    out_ref[...] = jnp.zeros(out_ref.shape, out_ref.dtype)
    for i in range(slot_count):
        home = home_ref[i]
        copies[i].wait()
        scores = (
            lax.dot_general(
                incoming_ref[home],
                cache_buf[i, 0],
                (((1,), (1,)), ((), ())),
                preferred_element_type=jnp.float32,
            )
            * scale
        )
        position = lax.broadcasted_iota(jnp.int32, scores.shape, 1)
        masked = jnp.where(position < len_ref[i], scores, -jnp.inf)
        peak = jnp.max(masked, axis=1, keepdims=True)
        weights = jnp.exp(masked - peak).astype(jnp.bfloat16)
        den = jnp.sum(weights.astype(jnp.float32), axis=1, keepdims=True)
        num = jnp.dot(weights, cache_buf[i, 1], preferred_element_type=jnp.float32)
        peak_low = peak.astype(jnp.bfloat16).astype(jnp.float32)
        shift = jnp.exp(peak - peak_low)
        shifted_den = den * shift
        den_high = shifted_den.astype(jnp.bfloat16).astype(jnp.float32)
        den_rest = shifted_den - den_high
        lane = lax.broadcasted_iota(jnp.int32, (rows, out_ref.shape[2]), 1)
        facts = jnp.where(
            lane == 0,
            peak_low,
            jnp.where(lane == 1, den_high, jnp.where(lane == 2, den_rest, 0.0)),
        )
        out_ref[home, :rows, :] = (num * shift).astype(out_ref.dtype)
        out_ref[home, rows:, :] = facts.astype(out_ref.dtype)


def slot_attention(home, cache_len, incoming, cache_kv, scale):
    groups, rows, width = incoming.shape
    slot_count, _, cache_size, _ = cache_kv.shape
    flops = 4 * slot_count * rows * cache_size * width
    moved = 2 * (cache_kv.size + incoming.size + 2 * groups * rows * width)
    return pl.pallas_call(
        functools.partial(slot_attention_kernel, scale=scale),
        out_shape=jax.ShapeDtypeStruct((groups, 2 * rows, width), incoming.dtype),
        in_specs=[
            pl.BlockSpec(memory_space=pltpu.SMEM),
            pl.BlockSpec(memory_space=pltpu.SMEM),
            pl.BlockSpec(memory_space=pltpu.VMEM),
            pl.BlockSpec(memory_space=pl.ANY),
        ],
        out_specs=pl.BlockSpec(memory_space=pltpu.VMEM),
        scratch_shapes=[
            pltpu.VMEM(cache_kv.shape, cache_kv.dtype),
            pltpu.SemaphoreType.DMA((slot_count,)),
        ],
        compiler_params=pltpu.CompilerParams(vmem_limit_bytes=16 * 1024 * 1024),
        cost_estimate=pl.CostEstimate(
            flops=flops, transcendentals=slot_count * rows * cache_size, bytes_accessed=moved
        ),
    )(home, cache_len, incoming, cache_kv)


def on_device(
    draft_hidden,
    q_weight,
    kv_weight,
    router_weight,
    routes,
    tree_mask,
    accepted,
    cache_kv,
    cache_len,
    slot_request,
):
    highest = lax.Precision.HIGHEST
    requests, drafts, part_width = draft_hidden.shape
    experts = q_weight.shape[0]
    head_width = q_weight.shape[2]
    head_count = head_width // HEAD_SIZE
    topk_count = routes.shape[2]
    kept_rows = accepted.shape[1]
    score_scale = HEAD_SIZE ** (-0.5)
    group_count = lax.axis_size("grp")
    group_idx = lax.axis_index("grp")
    slot_count = cache_kv.shape[0]
    cache_size = cache_kv.shape[2]

    row_pick = accepted[:, :, None] == jnp.arange(drafts, dtype=jnp.int32)[None, None, :]
    acc_part = jnp.einsum(
        "rat,rtd->rad",
        row_pick.astype(draft_hidden.dtype),
        draft_hidden,
        preferred_element_type=jnp.float32,
    ).astype(draft_hidden.dtype)
    acc_routes = jnp.sum(jnp.where(row_pick[..., None], routes[:, None], 0), axis=2)
    mask_rows = jnp.sum(jnp.where(row_pick[..., None], tree_mask[:, None], 0), axis=2)
    acc_mask = jnp.sum(jnp.where(row_pick[:, None, :, :], mask_rows[:, :, None, :], 0), axis=3)
    order = jnp.arange(kept_rows, dtype=jnp.int32)
    repeated = jnp.any(
        (accepted[:, :, None] == accepted[:, None, :]) & (order[None, None, :] < order[None, :, None]),
        axis=2,
    )
    usable_keys = (acc_mask > 0) & ~repeated[:, None, :]

    model_count = lax.axis_size("mdl")
    hidden_parts = lax.all_to_all(
        jnp.broadcast_to(acc_part[None], (model_count,) + acc_part.shape),
        "mdl",
        0,
        0,
        tiled=True,
    )
    acc_hidden = hidden_parts.transpose(1, 2, 0, 3).reshape(
        requests, kept_rows, model_count * part_width
    )

    q_sum = jnp.einsum("rad,edw->raew", acc_hidden, q_weight, preferred_element_type=jnp.float32)
    kv_sum = jnp.einsum("rtd,cdw->rtcw", acc_hidden, kv_weight, preferred_element_type=jnp.float32)
    logit_sum = jnp.einsum(
        "rad,de->rae", acc_hidden.astype(jnp.float32), router_weight, precision=highest
    )
    chosen_mask = acc_routes[..., None] == jnp.arange(experts, dtype=jnp.int32)
    chosen = jnp.sum(jnp.where(chosen_mask, logit_sum[:, :, None, :], 0.0), axis=3)
    gate_probs = jax.nn.softmax(chosen, axis=-1)
    queries = jnp.sum(jnp.where(chosen_mask[..., None], q_sum[:, :, None], 0.0), axis=3)
    queries = queries.astype(jnp.bfloat16)
    draft_keys = kv_sum[:, :, 0].astype(jnp.bfloat16)
    draft_values = kv_sum[:, :, 1].astype(jnp.bfloat16)

    tree_scores = (
        jnp.einsum("rakw,rjw->rakj", queries, draft_keys, preferred_element_type=jnp.float32)
        * score_scale
    )
    tree_peak, tree_den, tree_num = softmax_piece(
        tree_scores, usable_keys[:, :, None, :], draft_values, "rakj,rjw->rakw"
    )

    slot_table = slot_request.reshape(group_count, slot_count)
    home_of = slot_table // requests
    local_of = slot_table % requests
    mine = home_of == group_idx
    picked = jnp.sum(jnp.where(mine, local_of, 0), axis=1)
    any_mine = jnp.any(mine, axis=1)
    query_rows = queries.reshape(requests, kept_rows * topk_count, head_width)
    send_pick = (
        any_mine[:, None] & (picked[:, None] == jnp.arange(requests, dtype=jnp.int32)[None, :])
    ).astype(query_rows.dtype)
    outgoing = jnp.einsum(
        "dr,rxw->dxw", send_pick, query_rows, preferred_element_type=jnp.float32
    ).astype(query_rows.dtype)
    incoming = lax.all_to_all(outgoing, "grp", 0, 0, tiled=True)

    my_slots = lax.dynamic_slice_in_dim(slot_request, group_idx * slot_count, slot_count)
    row_count = kept_rows * topk_count
    returning = slot_attention(my_slots // requests, cache_len, incoming, cache_kv, score_scale)
    back = lax.all_to_all(returning, "grp", 0, 0, tiled=True)
    back_num = back[:, :row_count].astype(jnp.float32).reshape(
        group_count, kept_rows, topk_count, head_width
    )
    back_facts = back[:, row_count:, :3].astype(jnp.float32)
    back_peak = back_facts[..., 0].reshape(group_count, kept_rows, topk_count)
    back_den = (back_facts[..., 1] + back_facts[..., 2]).reshape(group_count, kept_rows, topk_count)

    home_ids = group_idx * requests + jnp.arange(requests, dtype=jnp.int32)
    matched = jnp.any(slot_table[None, :, :] == home_ids[:, None, None], axis=2)
    candidate = jnp.where(matched[:, :, None, None], back_peak[None], -jnp.inf)
    running_max = jnp.maximum(tree_peak, jnp.max(candidate, axis=1))
    rescale = jnp.exp(tree_peak - running_max)
    weight = jnp.exp(candidate - running_max[:, None])
    denominator = tree_den * rescale + jnp.sum(weight * back_den[None], axis=1)
    numerator = tree_num * rescale[..., None] + jnp.sum(
        weight[..., None] * back_num[None], axis=1
    )
    mixed = gate_probs[..., None] * numerator / denominator[..., None]
    return mixed.reshape(requests, kept_rows, topk_count, head_width).astype(jnp.bfloat16)


def solution(mesh):
    in_specs = (
        P("grp", None, "mdl"),
        P(None, None, "mdl"),
        P(None, None, "mdl"),
        P(),
        P("grp", None, None),
        P("grp", None, None),
        P("grp", None),
        P("grp", None, None, "mdl"),
        P("grp"),
        P(),
    )
    out_specs = P("grp", None, None, "mdl")
    return jax.shard_map(
        on_device, mesh=mesh, in_specs=in_specs, out_specs=out_specs, check_vma=False
    )
```

```python
import jax
import jax.numpy as jnp
import functools

from jax import lax
from jax.experimental import pallas as pl
from jax.experimental.pallas import tpu as pltpu
from jax.sharding import PartitionSpec as P

HEAD_SIZE = 128


def softmax_piece(scores, usable, values, contract):
    masked = jnp.where(usable, scores, -jnp.inf)
    peak_score = jnp.max(masked, axis=-1)
    weights_low = jnp.exp(masked - peak_score[..., None]).astype(jnp.bfloat16)
    denominator = jnp.sum(weights_low.astype(jnp.float32), axis=-1)
    numerator = jnp.einsum(contract, weights_low, values, preferred_element_type=jnp.float32)
    return (peak_score, denominator, numerator)


def slot_attention_kernel(
    home_ref, len_ref, incoming_ref, cache_hbm, out_ref, cache_buf, sems, *, scale
):
    slot_count = cache_buf.shape[0]
    rows = incoming_ref.shape[1]
    copies = [
        pltpu.make_async_copy(cache_hbm.at[i], cache_buf.at[i], sems.at[i])
        for i in range(slot_count)
    ]
    for copy in copies:
        copy.start()
    out_ref[...] = jnp.zeros(out_ref.shape, out_ref.dtype)
    for i in range(slot_count):
        home = home_ref[i]
        copies[i].wait()
        scores = (
            lax.dot_general(
                incoming_ref[home],
                cache_buf[i, 0],
                (((1,), (1,)), ((), ())),
                preferred_element_type=jnp.float32,
            )
            * scale
        )
        position = lax.broadcasted_iota(jnp.int32, scores.shape, 1)
        masked = jnp.where(position < len_ref[i], scores, -jnp.inf)
        peak = jnp.max(masked, axis=1, keepdims=True)
        weights = jnp.exp(masked - peak).astype(jnp.bfloat16)
        den = jnp.sum(weights.astype(jnp.float32), axis=1, keepdims=True)
        num = jnp.dot(weights, cache_buf[i, 1], preferred_element_type=jnp.float32)
        peak_low = peak.astype(jnp.bfloat16).astype(jnp.float32)
        shift = jnp.exp(peak - peak_low)
        shifted_den = den * shift
        den_high = shifted_den.astype(jnp.bfloat16).astype(jnp.float32)
        den_rest = shifted_den - den_high
        lane = lax.broadcasted_iota(jnp.int32, (rows, out_ref.shape[2]), 1)
        facts = jnp.where(
            lane == 0,
            peak_low,
            jnp.where(lane == 1, den_high, jnp.where(lane == 2, den_rest, 0.0)),
        )
        out_ref[home, :rows, :] = (num * shift).astype(out_ref.dtype)
        out_ref[home, rows:, :] = facts.astype(out_ref.dtype)


def slot_attention(home, cache_len, incoming, cache_kv, scale):
    groups, rows, width = incoming.shape
    slot_count, _, cache_size, _ = cache_kv.shape
    flops = 4 * slot_count * rows * cache_size * width
    moved = 2 * (cache_kv.size + incoming.size + 2 * groups * rows * width)
    return pl.pallas_call(
        functools.partial(slot_attention_kernel, scale=scale),
        out_shape=jax.ShapeDtypeStruct((groups, 2 * rows, width), incoming.dtype),
        in_specs=[
            pl.BlockSpec(memory_space=pltpu.SMEM),
            pl.BlockSpec(memory_space=pltpu.SMEM),
            pl.BlockSpec(memory_space=pltpu.VMEM),
            pl.BlockSpec(memory_space=pl.ANY),
        ],
        out_specs=pl.BlockSpec(memory_space=pltpu.VMEM),
        scratch_shapes=[
            pltpu.VMEM(cache_kv.shape, cache_kv.dtype),
            pltpu.SemaphoreType.DMA((slot_count,)),
        ],
        compiler_params=pltpu.CompilerParams(vmem_limit_bytes=16 * 1024 * 1024),
        cost_estimate=pl.CostEstimate(
            flops=flops, transcendentals=slot_count * rows * cache_size, bytes_accessed=moved
        ),
    )(home, cache_len, incoming, cache_kv)


def on_device(
    draft_hidden,
    q_weight,
    kv_weight,
    router_weight,
    routes,
    tree_mask,
    accepted,
    cache_kv,
    cache_len,
    slot_request,
):
    highest = lax.Precision.HIGHEST
    requests, drafts, part_width = draft_hidden.shape
    experts = q_weight.shape[0]
    head_width = q_weight.shape[2]
    head_count = head_width // HEAD_SIZE
    topk_count = routes.shape[2]
    kept_rows = accepted.shape[1]
    score_scale = HEAD_SIZE ** (-0.5)
    group_count = lax.axis_size("grp")
    group_idx = lax.axis_index("grp")
    slot_count = cache_kv.shape[0]
    cache_size = cache_kv.shape[2]

    row_pick = accepted[:, :, None] == jnp.arange(drafts, dtype=jnp.int32)[None, None, :]
    acc_part = jnp.einsum(
        "rat,rtd->rad",
        row_pick.astype(draft_hidden.dtype),
        draft_hidden,
        preferred_element_type=jnp.float32,
    ).astype(draft_hidden.dtype)
    acc_routes = jnp.sum(jnp.where(row_pick[..., None], routes[:, None], 0), axis=2)
    mask_rows = jnp.sum(jnp.where(row_pick[..., None], tree_mask[:, None], 0), axis=2)
    acc_mask = jnp.sum(jnp.where(row_pick[:, None, :, :], mask_rows[:, :, None, :], 0), axis=3)
    order = jnp.arange(kept_rows, dtype=jnp.int32)
    repeated = jnp.any(
        (accepted[:, :, None] == accepted[:, None, :]) & (order[None, None, :] < order[None, :, None]),
        axis=2,
    )
    usable_keys = (acc_mask > 0) & ~repeated[:, None, :]

    model_count = lax.axis_size("mdl")
    hidden_parts = lax.all_to_all(
        jnp.broadcast_to(acc_part[None], (model_count,) + acc_part.shape),
        "mdl",
        0,
        0,
        tiled=True,
    )
    acc_hidden = hidden_parts.transpose(1, 2, 0, 3).reshape(
        requests, kept_rows, model_count * part_width
    )

    q_sum = jnp.einsum("rad,edw->raew", acc_hidden, q_weight, preferred_element_type=jnp.float32)
    kv_sum = jnp.einsum("rtd,cdw->rtcw", acc_hidden, kv_weight, preferred_element_type=jnp.float32)
    logit_sum = jnp.einsum(
        "rad,de->rae", acc_hidden.astype(jnp.float32), router_weight, precision=highest
    )
    chosen_mask = acc_routes[..., None] == jnp.arange(experts, dtype=jnp.int32)
    chosen = jnp.sum(jnp.where(chosen_mask, logit_sum[:, :, None, :], 0.0), axis=3)
    gate_probs = jax.nn.softmax(chosen, axis=-1)
    queries = jnp.sum(jnp.where(chosen_mask[..., None], q_sum[:, :, None], 0.0), axis=3)
    queries = queries.astype(jnp.bfloat16)
    draft_keys = kv_sum[:, :, 0].astype(jnp.bfloat16)
    draft_values = kv_sum[:, :, 1].astype(jnp.bfloat16)

    tree_scores = (
        jnp.einsum("rakw,rjw->rakj", queries, draft_keys, preferred_element_type=jnp.float32)
        * score_scale
    )
    tree_peak, tree_den, tree_num = softmax_piece(
        tree_scores, usable_keys[:, :, None, :], draft_values, "rakj,rjw->rakw"
    )

    slot_table = slot_request.reshape(group_count, slot_count)
    home_of = slot_table // requests
    local_of = slot_table % requests
    mine = home_of == group_idx
    picked = jnp.sum(jnp.where(mine, local_of, 0), axis=1)
    any_mine = jnp.any(mine, axis=1)
    query_rows = queries.reshape(requests, kept_rows * topk_count, head_width)
    send_pick = (
        any_mine[:, None] & (picked[:, None] == jnp.arange(requests, dtype=jnp.int32)[None, :])
    ).astype(query_rows.dtype)
    outgoing = jnp.einsum(
        "dr,rxw->dxw", send_pick, query_rows, preferred_element_type=jnp.float32
    ).astype(query_rows.dtype)
    incoming = lax.all_to_all(outgoing, "grp", 0, 0, tiled=True)

    my_slots = lax.dynamic_slice_in_dim(slot_request, group_idx * slot_count, slot_count)
    row_count = kept_rows * topk_count
    returning = slot_attention(my_slots // requests, cache_len, incoming, cache_kv, score_scale)
    back = lax.all_to_all(returning, "grp", 0, 0, tiled=True)
    serving = jnp.any(home_of == group_idx, axis=1)
    place = jnp.cumsum(serving.astype(jnp.int32)) - 1
    source_pick = serving[None, :] & (
        place[None, :] == jnp.arange(slot_count, dtype=jnp.int32)[:, None]
    )
    source_valid = jnp.any(source_pick, axis=1)
    source_request = jnp.sum(
        jnp.where(source_pick, jnp.sum(jnp.where(mine, local_of, 0), axis=1)[None, :], 0), axis=1
    )
    chosen_blocks = (
        jnp.einsum(
            "kd,dx->kx",
            source_pick.astype(back.dtype),
            back.reshape(group_count, -1),
            preferred_element_type=jnp.float32,
        )
        .reshape(slot_count, 2 * row_count, head_width)
    )
    back_num = chosen_blocks[:, :row_count].reshape(slot_count, kept_rows, topk_count, head_width)
    back_facts = chosen_blocks[:, row_count:, :3]
    back_peak = back_facts[..., 0].reshape(slot_count, kept_rows, topk_count)
    back_den = (back_facts[..., 1] + back_facts[..., 2]).reshape(slot_count, kept_rows, topk_count)

    matched = (
        source_valid[None, :]
        & (source_request[None, :] == jnp.arange(requests, dtype=jnp.int32)[:, None])
    )
    candidate = jnp.where(matched[:, :, None, None], back_peak[None], -jnp.inf)
    running_max = jnp.maximum(tree_peak, jnp.max(candidate, axis=1))
    rescale = jnp.exp(tree_peak - running_max)
    weight = jnp.exp(candidate - running_max[:, None])
    denominator = tree_den * rescale + jnp.sum(weight * back_den[None], axis=1)
    numerator = tree_num * rescale[..., None] + jnp.sum(
        weight[..., None] * back_num[None], axis=1
    )
    mixed = gate_probs[..., None] * numerator / denominator[..., None]
    return mixed.reshape(requests, kept_rows, topk_count, head_width).astype(jnp.bfloat16)


def solution(mesh):
    in_specs = (
        P("grp", None, "mdl"),
        P(None, None, "mdl"),
        P(None, None, "mdl"),
        P(),
        P("grp", None, None),
        P("grp", None, None),
        P("grp", None),
        P("grp", None, None, "mdl"),
        P("grp"),
        P(),
    )
    out_specs = P("grp", None, None, "mdl")
    return jax.shard_map(
        on_device, mesh=mesh, in_specs=in_specs, out_specs=out_specs, check_vma=False
    )
```

```python
import jax
import jax.numpy as jnp
import functools

from jax import lax
from jax.experimental import pallas as pl
from jax.experimental.pallas import tpu as pltpu
from jax.sharding import PartitionSpec as P

HEAD_SIZE = 128


def softmax_piece(scores, usable, values, contract):
    masked = jnp.where(usable, scores, -jnp.inf)
    peak_score = jnp.max(masked, axis=-1)
    weights_low = jnp.exp(masked - peak_score[..., None]).astype(jnp.bfloat16)
    denominator = jnp.sum(weights_low.astype(jnp.float32), axis=-1)
    numerator = jnp.einsum(contract, weights_low, values, preferred_element_type=jnp.float32)
    return (peak_score, denominator, numerator)


def slot_attention_kernel(
    home_ref, len_ref, incoming_ref, cache_hbm, out_ref, cache_buf, sems, *, scale
):
    slot_count = cache_buf.shape[0]
    rows = incoming_ref.shape[1]
    copies = [
        pltpu.make_async_copy(cache_hbm.at[i], cache_buf.at[i], sems.at[i])
        for i in range(slot_count)
    ]
    for copy in copies:
        copy.start()
    out_ref[...] = jnp.zeros(out_ref.shape, out_ref.dtype)
    for i in range(slot_count):
        home = home_ref[i]
        copies[i].wait()
        scores = (
            lax.dot_general(
                incoming_ref[home],
                cache_buf[i, 0],
                (((1,), (1,)), ((), ())),
                preferred_element_type=jnp.float32,
            )
            * scale
        )
        position = lax.broadcasted_iota(jnp.int32, scores.shape, 1)
        masked = jnp.where(position < len_ref[i], scores, -jnp.inf)
        peak = jnp.max(masked, axis=1, keepdims=True)
        weights = jnp.exp(masked - peak).astype(jnp.bfloat16)
        den = jnp.sum(weights.astype(jnp.float32), axis=1, keepdims=True)
        num = jnp.dot(weights, cache_buf[i, 1], preferred_element_type=jnp.float32)
        peak_low = peak.astype(jnp.bfloat16).astype(jnp.float32)
        shift = jnp.exp(peak - peak_low)
        shifted_den = den * shift
        den_high = shifted_den.astype(jnp.bfloat16).astype(jnp.float32)
        den_rest = shifted_den - den_high
        lane = lax.broadcasted_iota(jnp.int32, (rows, out_ref.shape[2]), 1)
        facts = jnp.where(
            lane == 0,
            peak_low,
            jnp.where(lane == 1, den_high, jnp.where(lane == 2, den_rest, 0.0)),
        )
        out_ref[home, :rows, :] = (num * shift).astype(out_ref.dtype)
        out_ref[home, rows:, :] = facts.astype(out_ref.dtype)


def slot_attention(home, cache_len, incoming, cache_kv, scale):
    groups, rows, width = incoming.shape
    slot_count, _, cache_size, _ = cache_kv.shape
    flops = 4 * slot_count * rows * cache_size * width
    moved = 2 * (cache_kv.size + incoming.size + 2 * groups * rows * width)
    return pl.pallas_call(
        functools.partial(slot_attention_kernel, scale=scale),
        out_shape=jax.ShapeDtypeStruct((groups, 2 * rows, width), incoming.dtype),
        in_specs=[
            pl.BlockSpec(memory_space=pltpu.SMEM),
            pl.BlockSpec(memory_space=pltpu.SMEM),
            pl.BlockSpec(memory_space=pltpu.VMEM),
            pl.BlockSpec(memory_space=pl.ANY),
        ],
        out_specs=pl.BlockSpec(memory_space=pltpu.VMEM),
        scratch_shapes=[
            pltpu.VMEM(cache_kv.shape, cache_kv.dtype),
            pltpu.SemaphoreType.DMA((slot_count,)),
        ],
        compiler_params=pltpu.CompilerParams(vmem_limit_bytes=16 * 1024 * 1024),
        cost_estimate=pl.CostEstimate(
            flops=flops, transcendentals=slot_count * rows * cache_size, bytes_accessed=moved
        ),
    )(home, cache_len, incoming, cache_kv)


def on_device(
    draft_hidden,
    q_weight,
    kv_weight,
    router_weight,
    routes,
    tree_mask,
    accepted,
    cache_kv,
    cache_len,
    slot_request,
):
    highest = lax.Precision.HIGHEST
    requests, drafts, part_width = draft_hidden.shape
    experts = q_weight.shape[0]
    head_width = q_weight.shape[2]
    head_count = head_width // HEAD_SIZE
    topk_count = routes.shape[2]
    kept_rows = accepted.shape[1]
    score_scale = HEAD_SIZE ** (-0.5)
    group_count = lax.axis_size("grp")
    group_idx = lax.axis_index("grp")
    slot_count = cache_kv.shape[0]
    cache_size = cache_kv.shape[2]

    row_pick = accepted[:, :, None] == jnp.arange(drafts, dtype=jnp.int32)[None, None, :]
    acc_part = jnp.einsum(
        "rat,rtd->rad",
        row_pick.astype(draft_hidden.dtype),
        draft_hidden,
        preferred_element_type=jnp.float32,
    ).astype(draft_hidden.dtype)
    acc_routes = jnp.sum(jnp.where(row_pick[..., None], routes[:, None], 0), axis=2)
    mask_rows = jnp.sum(jnp.where(row_pick[..., None], tree_mask[:, None], 0), axis=2)
    acc_mask = jnp.sum(jnp.where(row_pick[:, None, :, :], mask_rows[:, :, None, :], 0), axis=3)
    order = jnp.arange(kept_rows, dtype=jnp.int32)
    repeated = jnp.any(
        (accepted[:, :, None] == accepted[:, None, :]) & (order[None, None, :] < order[None, :, None]),
        axis=2,
    )
    usable_keys = (acc_mask > 0) & ~repeated[:, None, :]

    model_count = lax.axis_size("mdl")
    hidden_parts = lax.all_to_all(
        jnp.broadcast_to(acc_part[None], (model_count,) + acc_part.shape),
        "mdl",
        0,
        0,
        tiled=True,
    )
    acc_hidden = hidden_parts.transpose(1, 2, 0, 3).reshape(
        requests, kept_rows, model_count * part_width
    )

    q_sum = jnp.einsum("rad,edw->raew", acc_hidden, q_weight, preferred_element_type=jnp.float32)
    kv_sum = jnp.einsum("rtd,cdw->rtcw", acc_hidden, kv_weight, preferred_element_type=jnp.float32)
    logit_sum = jnp.einsum(
        "rad,de->rae", acc_hidden.astype(jnp.float32), router_weight, precision=highest
    )
    chosen_mask = acc_routes[..., None] == jnp.arange(experts, dtype=jnp.int32)
    chosen = jnp.sum(jnp.where(chosen_mask, logit_sum[:, :, None, :], 0.0), axis=3)
    gate_probs = jax.nn.softmax(chosen, axis=-1)
    queries = jnp.sum(jnp.where(chosen_mask[..., None], q_sum[:, :, None], 0.0), axis=3)
    queries = queries.astype(jnp.bfloat16)
    draft_keys = kv_sum[:, :, 0].astype(jnp.bfloat16)
    draft_values = kv_sum[:, :, 1].astype(jnp.bfloat16)

    tree_scores = (
        jnp.einsum("rakw,rjw->rakj", queries, draft_keys, preferred_element_type=jnp.float32)
        * score_scale
    )
    tree_peak, tree_den, tree_num = softmax_piece(
        tree_scores, usable_keys[:, :, None, :], draft_values, "rakj,rjw->rakw"
    )

    slot_table = slot_request.reshape(group_count, slot_count)
    home_of = slot_table // requests
    local_of = slot_table % requests
    mine = home_of == group_idx
    picked = jnp.sum(jnp.where(mine, local_of, 0), axis=1)
    any_mine = jnp.any(mine, axis=1)
    query_rows = queries.reshape(requests, kept_rows * topk_count, head_width)
    send_pick = (
        any_mine[:, None] & (picked[:, None] == jnp.arange(requests, dtype=jnp.int32)[None, :])
    ).astype(query_rows.dtype)
    outgoing = jnp.einsum(
        "dr,rxw->dxw", send_pick, query_rows, preferred_element_type=jnp.float32
    ).astype(query_rows.dtype)
    incoming = lax.all_to_all(outgoing, "grp", 0, 0, tiled=True)

    my_slots = lax.dynamic_slice_in_dim(slot_request, group_idx * slot_count, slot_count)
    row_count = kept_rows * topk_count
    returning = slot_attention(my_slots // requests, cache_len, incoming, cache_kv, score_scale)
    back = lax.all_to_all(returning, "grp", 0, 0, tiled=True)
    serving = jnp.any(home_of == group_idx, axis=1)
    place = jnp.cumsum(serving.astype(jnp.int32)) - 1
    source_pick = serving[None, :] & (
        place[None, :] == jnp.arange(slot_count, dtype=jnp.int32)[:, None]
    )
    source_valid = jnp.any(source_pick, axis=1)
    source_request = jnp.sum(
        jnp.where(source_pick, jnp.sum(jnp.where(mine, local_of, 0), axis=1)[None, :], 0), axis=1
    )
    source_index = jnp.sum(
        jnp.where(source_pick, jnp.arange(group_count, dtype=jnp.int32)[None, :], 0), axis=1
    )
    chosen_blocks = jnp.stack(
        [lax.dynamic_index_in_dim(back, source_index[k], 0, keepdims=False) for k in range(slot_count)]
    ).astype(jnp.float32)
    back_num = chosen_blocks[:, :row_count].reshape(slot_count, kept_rows, topk_count, head_width)
    back_facts = chosen_blocks[:, row_count:, :3]
    back_peak = back_facts[..., 0].reshape(slot_count, kept_rows, topk_count)
    back_den = (back_facts[..., 1] + back_facts[..., 2]).reshape(slot_count, kept_rows, topk_count)

    matched = (
        source_valid[None, :]
        & (source_request[None, :] == jnp.arange(requests, dtype=jnp.int32)[:, None])
    )
    candidate = jnp.where(matched[:, :, None, None], back_peak[None], -jnp.inf)
    running_max = jnp.maximum(tree_peak, jnp.max(candidate, axis=1))
    rescale = jnp.exp(tree_peak - running_max)
    weight = jnp.exp(candidate - running_max[:, None])
    denominator = tree_den * rescale + jnp.sum(weight * back_den[None], axis=1)
    numerator = tree_num * rescale[..., None] + jnp.sum(
        weight[..., None] * back_num[None], axis=1
    )
    mixed = gate_probs[..., None] * numerator / denominator[..., None]
    return mixed.reshape(requests, kept_rows, topk_count, head_width).astype(jnp.bfloat16)


def solution(mesh):
    in_specs = (
        P("grp", None, "mdl"),
        P(None, None, "mdl"),
        P(None, None, "mdl"),
        P(),
        P("grp", None, None),
        P("grp", None, None),
        P("grp", None),
        P("grp", None, None, "mdl"),
        P("grp"),
        P(),
    )
    out_specs = P("grp", None, None, "mdl")
    return jax.shard_map(
        on_device, mesh=mesh, in_specs=in_specs, out_specs=out_specs, check_vma=False
    )
```

```python
import jax
import jax.numpy as jnp
import functools

from jax import lax
from jax.experimental import pallas as pl
from jax.experimental.pallas import tpu as pltpu
from jax.sharding import PartitionSpec as P

HEAD_SIZE = 128


def softmax_piece(scores, usable, values, contract):
    masked = jnp.where(usable, scores, -jnp.inf)
    peak_score = jnp.max(masked, axis=-1)
    weights_low = jnp.exp(masked - peak_score[..., None]).astype(jnp.bfloat16)
    denominator = jnp.sum(weights_low.astype(jnp.float32), axis=-1)
    numerator = jnp.einsum(contract, weights_low, values, preferred_element_type=jnp.float32)
    return (peak_score, denominator, numerator)


def slot_attention_kernel(home_ref, len_ref, incoming_ref, cache_ref, out_ref, *, scale):
    slot_count = cache_ref.shape[0]
    rows = incoming_ref.shape[1]
    out_ref[...] = jnp.zeros(out_ref.shape, out_ref.dtype)
    for i in range(slot_count):
        home = home_ref[i]
        scores = (
            lax.dot_general(
                incoming_ref[home],
                cache_ref[i, 0],
                (((1,), (1,)), ((), ())),
                preferred_element_type=jnp.float32,
            )
            * scale
        )
        position = lax.broadcasted_iota(jnp.int32, scores.shape, 1)
        masked = jnp.where(position < len_ref[i], scores, -jnp.inf)
        peak = jnp.max(masked, axis=1, keepdims=True)
        weights = jnp.exp(masked - peak).astype(jnp.bfloat16)
        den = jnp.sum(weights.astype(jnp.float32), axis=1, keepdims=True)
        num = jnp.dot(weights, cache_ref[i, 1], preferred_element_type=jnp.float32)
        peak_low = peak.astype(jnp.bfloat16).astype(jnp.float32)
        shift = jnp.exp(peak - peak_low)
        shifted_den = den * shift
        den_high = shifted_den.astype(jnp.bfloat16).astype(jnp.float32)
        den_rest = shifted_den - den_high
        lane = lax.broadcasted_iota(jnp.int32, (rows, out_ref.shape[2]), 1)
        facts = jnp.where(
            lane == 0,
            peak_low,
            jnp.where(lane == 1, den_high, jnp.where(lane == 2, den_rest, 0.0)),
        )
        out_ref[home, :rows, :] = (num * shift).astype(out_ref.dtype)
        out_ref[home, rows:, :] = facts.astype(out_ref.dtype)


def slot_attention(home, cache_len, incoming, cache_kv, scale):
    groups, rows, width = incoming.shape
    slot_count, _, cache_size, _ = cache_kv.shape
    flops = 4 * slot_count * rows * cache_size * width
    moved = 2 * (cache_kv.size + incoming.size + 2 * groups * rows * width)
    return pl.pallas_call(
        functools.partial(slot_attention_kernel, scale=scale),
        out_shape=jax.ShapeDtypeStruct((groups, 2 * rows, width), incoming.dtype),
        in_specs=[
            pl.BlockSpec(memory_space=pltpu.SMEM),
            pl.BlockSpec(memory_space=pltpu.SMEM),
            pl.BlockSpec(memory_space=pltpu.VMEM),
            pl.BlockSpec(memory_space=pltpu.VMEM),
        ],
        out_specs=pl.BlockSpec(memory_space=pltpu.VMEM),
        cost_estimate=pl.CostEstimate(
            flops=flops, transcendentals=slot_count * rows * cache_size, bytes_accessed=moved
        ),
    )(home, cache_len, incoming, cache_kv)


def on_device(
    draft_hidden,
    q_weight,
    kv_weight,
    router_weight,
    routes,
    tree_mask,
    accepted,
    cache_kv,
    cache_len,
    slot_request,
):
    highest = lax.Precision.HIGHEST
    requests, drafts, part_width = draft_hidden.shape
    experts = q_weight.shape[0]
    head_width = q_weight.shape[2]
    head_count = head_width // HEAD_SIZE
    topk_count = routes.shape[2]
    kept_rows = accepted.shape[1]
    score_scale = HEAD_SIZE ** (-0.5)
    group_count = lax.axis_size("grp")
    group_idx = lax.axis_index("grp")
    slot_count = cache_kv.shape[0]
    cache_size = cache_kv.shape[2]

    row_pick = accepted[:, :, None] == jnp.arange(drafts, dtype=jnp.int32)[None, None, :]
    acc_part = jnp.einsum(
        "rat,rtd->rad",
        row_pick.astype(draft_hidden.dtype),
        draft_hidden,
        preferred_element_type=jnp.float32,
    ).astype(draft_hidden.dtype)
    acc_routes = jnp.sum(jnp.where(row_pick[..., None], routes[:, None], 0), axis=2)
    mask_rows = jnp.sum(jnp.where(row_pick[..., None], tree_mask[:, None], 0), axis=2)
    acc_mask = jnp.sum(jnp.where(row_pick[:, None, :, :], mask_rows[:, :, None, :], 0), axis=3)
    order = jnp.arange(kept_rows, dtype=jnp.int32)
    repeated = jnp.any(
        (accepted[:, :, None] == accepted[:, None, :]) & (order[None, None, :] < order[None, :, None]),
        axis=2,
    )
    usable_keys = (acc_mask > 0) & ~repeated[:, None, :]

    model_count = lax.axis_size("mdl")
    hidden_parts = lax.all_to_all(
        jnp.broadcast_to(acc_part[None], (model_count,) + acc_part.shape),
        "mdl",
        0,
        0,
        tiled=True,
    )
    acc_hidden = hidden_parts.transpose(1, 2, 0, 3).reshape(
        requests, kept_rows, model_count * part_width
    )

    q_sum = jnp.einsum("rad,edw->raew", acc_hidden, q_weight, preferred_element_type=jnp.float32)
    kv_sum = jnp.einsum("rtd,cdw->rtcw", acc_hidden, kv_weight, preferred_element_type=jnp.float32)
    logit_sum = jnp.einsum(
        "rad,de->rae", acc_hidden.astype(jnp.float32), router_weight, precision=highest
    )
    chosen_mask = acc_routes[..., None] == jnp.arange(experts, dtype=jnp.int32)
    chosen = jnp.sum(jnp.where(chosen_mask, logit_sum[:, :, None, :], 0.0), axis=3)
    gate_probs = jax.nn.softmax(chosen, axis=-1)
    queries = jnp.sum(jnp.where(chosen_mask[..., None], q_sum[:, :, None], 0.0), axis=3)
    queries = queries.astype(jnp.bfloat16)
    draft_keys = kv_sum[:, :, 0].astype(jnp.bfloat16)
    draft_values = kv_sum[:, :, 1].astype(jnp.bfloat16)

    tree_scores = (
        jnp.einsum("rakw,rjw->rakj", queries, draft_keys, preferred_element_type=jnp.float32)
        * score_scale
    )
    tree_peak, tree_den, tree_num = softmax_piece(
        tree_scores, usable_keys[:, :, None, :], draft_values, "rakj,rjw->rakw"
    )

    slot_table = slot_request.reshape(group_count, slot_count)
    home_of = slot_table // requests
    local_of = slot_table % requests
    mine = home_of == group_idx
    picked = jnp.sum(jnp.where(mine, local_of, 0), axis=1)
    any_mine = jnp.any(mine, axis=1)
    query_rows = queries.reshape(requests, kept_rows * topk_count, head_width)
    outgoing = jnp.where(
        any_mine[:, None, None],
        jnp.where((picked == 1)[:, None, None], query_rows[1][None], query_rows[0][None]),
        jnp.zeros((), query_rows.dtype),
    )
    incoming = lax.all_to_all(outgoing, "grp", 0, 0, tiled=True)

    my_slots = lax.dynamic_slice_in_dim(slot_request, group_idx * slot_count, slot_count)
    row_count = kept_rows * topk_count
    returning = slot_attention(my_slots // requests, cache_len, incoming, cache_kv, score_scale)
    back = lax.all_to_all(returning, "grp", 0, 0, tiled=True)
    serving = jnp.any(home_of == group_idx, axis=1)
    place = jnp.cumsum(serving.astype(jnp.int32)) - 1
    source_pick = serving[None, :] & (
        place[None, :] == jnp.arange(slot_count, dtype=jnp.int32)[:, None]
    )
    source_valid = jnp.any(source_pick, axis=1)
    source_request = jnp.sum(
        jnp.where(source_pick, jnp.sum(jnp.where(mine, local_of, 0), axis=1)[None, :], 0), axis=1
    )
    chosen_blocks = (
        jnp.einsum(
            "kd,dx->kx",
            source_pick.astype(back.dtype),
            back.reshape(group_count, -1),
            preferred_element_type=jnp.float32,
        )
        .reshape(slot_count, 2 * row_count, head_width)
    )
    back_num = chosen_blocks[:, :row_count].reshape(slot_count, kept_rows, topk_count, head_width)
    back_facts = chosen_blocks[:, row_count:, :3]
    back_peak = back_facts[..., 0].reshape(slot_count, kept_rows, topk_count)
    back_den = (back_facts[..., 1] + back_facts[..., 2]).reshape(slot_count, kept_rows, topk_count)

    matched = (
        source_valid[None, :]
        & (source_request[None, :] == jnp.arange(requests, dtype=jnp.int32)[:, None])
    )
    candidate = jnp.where(matched[:, :, None, None], back_peak[None], -jnp.inf)
    running_max = jnp.maximum(tree_peak, jnp.max(candidate, axis=1))
    rescale = jnp.exp(tree_peak - running_max)
    weight = jnp.exp(candidate - running_max[:, None])
    denominator = tree_den * rescale + jnp.sum(weight * back_den[None], axis=1)
    numerator = tree_num * rescale[..., None] + jnp.sum(
        weight[..., None] * back_num[None], axis=1
    )
    mixed = gate_probs[..., None] * numerator / denominator[..., None]
    return mixed.reshape(requests, kept_rows, topk_count, head_width).astype(jnp.bfloat16)


def solution(mesh):
    in_specs = (
        P("grp", None, "mdl"),
        P(None, None, "mdl"),
        P(None, None, "mdl"),
        P(),
        P("grp", None, None),
        P("grp", None, None),
        P("grp", None),
        P("grp", None, None, "mdl"),
        P("grp"),
        P(),
    )
    out_specs = P("grp", None, None, "mdl")
    return jax.shard_map(
        on_device, mesh=mesh, in_specs=in_specs, out_specs=out_specs, check_vma=False
    )
```

```python
import jax
import jax.numpy as jnp
import functools

from jax import lax
from jax.experimental import pallas as pl
from jax.experimental.pallas import tpu as pltpu
from jax.sharding import PartitionSpec as P

HEAD_SIZE = 128


def softmax_piece(scores, usable, values, contract):
    masked = jnp.where(usable, scores, -jnp.inf)
    peak_score = jnp.max(masked, axis=-1)
    weights_low = jnp.exp(masked - peak_score[..., None]).astype(jnp.bfloat16)
    denominator = jnp.sum(weights_low.astype(jnp.float32), axis=-1)
    numerator = jnp.einsum(contract, weights_low, values, preferred_element_type=jnp.float32)
    return (peak_score, denominator, numerator)


def slot_attention_kernel(home_ref, len_ref, incoming_ref, cache_ref, out_ref, *, scale):
    slot_count = cache_ref.shape[0]
    rows = incoming_ref.shape[1]
    out_ref[...] = jnp.zeros(out_ref.shape, out_ref.dtype)
    for i in range(slot_count):
        home = home_ref[i]
        scores = (
            lax.dot_general(
                incoming_ref[home],
                cache_ref[i, 0],
                (((1,), (1,)), ((), ())),
                preferred_element_type=jnp.float32,
            )
            * scale
        )
        position = lax.broadcasted_iota(jnp.int32, scores.shape, 1)
        masked = jnp.where(position < len_ref[i], scores, -jnp.inf)
        peak = jnp.max(masked, axis=1, keepdims=True)
        weights = jnp.exp(masked - peak).astype(jnp.bfloat16)
        den = jnp.sum(weights.astype(jnp.float32), axis=1, keepdims=True)
        num = jnp.dot(weights, cache_ref[i, 1], preferred_element_type=jnp.float32)
        peak_low = peak.astype(jnp.bfloat16).astype(jnp.float32)
        shift = jnp.exp(peak - peak_low)
        shifted_den = den * shift
        den_high = shifted_den.astype(jnp.bfloat16).astype(jnp.float32)
        den_rest = shifted_den - den_high
        lane = lax.broadcasted_iota(jnp.int32, (rows, out_ref.shape[2]), 1)
        facts = jnp.where(
            lane == 0,
            peak_low,
            jnp.where(lane == 1, den_high, jnp.where(lane == 2, den_rest, 0.0)),
        )
        out_ref[home, :rows, :] = (num * shift).astype(out_ref.dtype)
        out_ref[home, rows:, :] = facts.astype(out_ref.dtype)


def slot_attention(home, cache_len, incoming, cache_kv, scale):
    groups, rows, width = incoming.shape
    slot_count, _, cache_size, _ = cache_kv.shape
    flops = 4 * slot_count * rows * cache_size * width
    moved = 2 * (cache_kv.size + incoming.size + 2 * groups * rows * width)
    return pl.pallas_call(
        functools.partial(slot_attention_kernel, scale=scale),
        out_shape=jax.ShapeDtypeStruct((groups, 2 * rows, width), incoming.dtype),
        in_specs=[
            pl.BlockSpec(memory_space=pltpu.SMEM),
            pl.BlockSpec(memory_space=pltpu.SMEM),
            pl.BlockSpec(memory_space=pltpu.VMEM),
            pl.BlockSpec(memory_space=pltpu.VMEM),
        ],
        out_specs=pl.BlockSpec(memory_space=pltpu.VMEM),
        cost_estimate=pl.CostEstimate(
            flops=flops, transcendentals=slot_count * rows * cache_size, bytes_accessed=moved
        ),
    )(home, cache_len, incoming, cache_kv)


def blend_kernel(
    index_ref, request_ref, back_ref, peak_ref, den_ref, num_ref, gate_ref, out_ref
):
    rows = num_ref.shape[1]
    for j in range(out_ref.shape[0]):
        blocks = []
        for k in range(index_ref.shape[0]):
            block = index_ref[k]
            serves = request_ref[k] == j
            blocks.append((block, serves, back_ref[block, rows:, 0:1].astype(jnp.float32)))
        running_max = peak_ref[j]
        for block, serves, peak in blocks:
            running_max = jnp.where(serves, jnp.maximum(running_max, peak), running_max)
        rescale = jnp.exp(peak_ref[j] - running_max)
        denominator = den_ref[j] * rescale
        numerator = num_ref[j] * rescale
        for block, serves, peak in blocks:
            weight = jnp.where(serves, jnp.exp(peak - running_max), 0.0)
            total = back_ref[block, rows:, 1:2].astype(jnp.float32) + back_ref[
                block, rows:, 2:3
            ].astype(jnp.float32)
            denominator = denominator + weight * total
            numerator = numerator + weight * back_ref[block, :rows, :].astype(jnp.float32)
        out_ref[j] = (gate_ref[j] * numerator / denominator).astype(out_ref.dtype)


def blend(index, request, back, peak, den, num, gate):
    smem = pl.BlockSpec(memory_space=pltpu.SMEM)
    vmem = pl.BlockSpec(memory_space=pltpu.VMEM)
    return pl.pallas_call(
        blend_kernel,
        out_shape=jax.ShapeDtypeStruct(num.shape, jnp.bfloat16),
        in_specs=[smem, smem, vmem, vmem, vmem, vmem, vmem],
        out_specs=vmem,
    )(index, request, back, peak, den, num, gate)


def on_device(
    draft_hidden,
    q_weight,
    kv_weight,
    router_weight,
    routes,
    tree_mask,
    accepted,
    cache_kv,
    cache_len,
    slot_request,
):
    highest = lax.Precision.HIGHEST
    requests, drafts, part_width = draft_hidden.shape
    experts = q_weight.shape[0]
    head_width = q_weight.shape[2]
    head_count = head_width // HEAD_SIZE
    topk_count = routes.shape[2]
    kept_rows = accepted.shape[1]
    score_scale = HEAD_SIZE ** (-0.5)
    group_count = lax.axis_size("grp")
    group_idx = lax.axis_index("grp")
    slot_count = cache_kv.shape[0]
    cache_size = cache_kv.shape[2]

    row_pick = accepted[:, :, None] == jnp.arange(drafts, dtype=jnp.int32)[None, None, :]
    acc_part = jnp.einsum(
        "rat,rtd->rad",
        row_pick.astype(draft_hidden.dtype),
        draft_hidden,
        preferred_element_type=jnp.float32,
    ).astype(draft_hidden.dtype)
    acc_routes = jnp.sum(jnp.where(row_pick[..., None], routes[:, None], 0), axis=2)
    mask_rows = jnp.sum(jnp.where(row_pick[..., None], tree_mask[:, None], 0), axis=2)
    acc_mask = jnp.sum(jnp.where(row_pick[:, None, :, :], mask_rows[:, :, None, :], 0), axis=3)
    order = jnp.arange(kept_rows, dtype=jnp.int32)
    repeated = jnp.any(
        (accepted[:, :, None] == accepted[:, None, :]) & (order[None, None, :] < order[None, :, None]),
        axis=2,
    )
    usable_keys = (acc_mask > 0) & ~repeated[:, None, :]

    model_count = lax.axis_size("mdl")
    hidden_parts = lax.all_to_all(
        jnp.broadcast_to(acc_part[None], (model_count,) + acc_part.shape),
        "mdl",
        0,
        0,
        tiled=True,
    )
    acc_hidden = hidden_parts.transpose(1, 2, 0, 3).reshape(
        requests, kept_rows, model_count * part_width
    )

    q_sum = jnp.einsum("rad,edw->raew", acc_hidden, q_weight, preferred_element_type=jnp.float32)
    kv_sum = jnp.einsum("rtd,cdw->rtcw", acc_hidden, kv_weight, preferred_element_type=jnp.float32)
    logit_sum = jnp.einsum(
        "rad,de->rae", acc_hidden.astype(jnp.float32), router_weight, precision=highest
    )
    chosen_mask = acc_routes[..., None] == jnp.arange(experts, dtype=jnp.int32)
    chosen = jnp.sum(jnp.where(chosen_mask, logit_sum[:, :, None, :], 0.0), axis=3)
    gate_probs = jax.nn.softmax(chosen, axis=-1)
    queries = jnp.sum(jnp.where(chosen_mask[..., None], q_sum[:, :, None], 0.0), axis=3)
    queries = queries.astype(jnp.bfloat16)
    draft_keys = kv_sum[:, :, 0].astype(jnp.bfloat16)
    draft_values = kv_sum[:, :, 1].astype(jnp.bfloat16)

    tree_scores = (
        jnp.einsum("rakw,rjw->rakj", queries, draft_keys, preferred_element_type=jnp.float32)
        * score_scale
    )
    tree_peak, tree_den, tree_num = softmax_piece(
        tree_scores, usable_keys[:, :, None, :], draft_values, "rakj,rjw->rakw"
    )

    slot_table = slot_request.reshape(group_count, slot_count)
    home_of = slot_table // requests
    local_of = slot_table % requests
    mine = home_of == group_idx
    picked = jnp.sum(jnp.where(mine, local_of, 0), axis=1)
    any_mine = jnp.any(mine, axis=1)
    query_rows = queries.reshape(requests, kept_rows * topk_count, head_width)
    outgoing = jnp.where(
        any_mine[:, None, None],
        jnp.where((picked == 1)[:, None, None], query_rows[1][None], query_rows[0][None]),
        jnp.zeros((), query_rows.dtype),
    )
    incoming = lax.all_to_all(outgoing, "grp", 0, 0, tiled=True)

    my_slots = lax.dynamic_slice_in_dim(slot_request, group_idx * slot_count, slot_count)
    row_count = kept_rows * topk_count
    returning = slot_attention(my_slots // requests, cache_len, incoming, cache_kv, score_scale)
    back = lax.all_to_all(returning, "grp", 0, 0, tiled=True)
    serving = jnp.any(home_of == group_idx, axis=1)
    place = jnp.cumsum(serving.astype(jnp.int32)) - 1
    source_pick = serving[None, :] & (
        place[None, :] == jnp.arange(slot_count, dtype=jnp.int32)[:, None]
    )
    source_valid = jnp.any(source_pick, axis=1)
    source_request = jnp.sum(
        jnp.where(source_pick, jnp.sum(jnp.where(mine, local_of, 0), axis=1)[None, :], 0), axis=1
    )
    source_index = jnp.sum(
        jnp.where(source_pick, jnp.arange(group_count, dtype=jnp.int32)[None, :], 0), axis=1
    )
    source_request = jnp.where(source_valid, source_request, -1)
    mixed = blend(
        source_index,
        source_request,
        back,
        tree_peak.reshape(requests, row_count, 1),
        tree_den.reshape(requests, row_count, 1),
        tree_num.reshape(requests, row_count, head_width),
        gate_probs.reshape(requests, row_count, 1),
    )
    return mixed.reshape(requests, kept_rows, topk_count, head_width).astype(jnp.bfloat16)


def solution(mesh):
    in_specs = (
        P("grp", None, "mdl"),
        P(None, None, "mdl"),
        P(None, None, "mdl"),
        P(),
        P("grp", None, None),
        P("grp", None, None),
        P("grp", None),
        P("grp", None, None, "mdl"),
        P("grp"),
        P(),
    )
    out_specs = P("grp", None, None, "mdl")
    return jax.shard_map(
        on_device, mesh=mesh, in_specs=in_specs, out_specs=out_specs, check_vma=False
    )
```

```python
import jax
import jax.numpy as jnp
import functools

from jax import lax
from jax.experimental import pallas as pl
from jax.experimental.pallas import tpu as pltpu
from jax.sharding import PartitionSpec as P

HEAD_SIZE = 128


def softmax_piece(scores, usable, values, contract):
    masked = jnp.where(usable, scores, -jnp.inf)
    peak_score = jnp.max(masked, axis=-1)
    weights_low = jnp.exp(masked - peak_score[..., None]).astype(jnp.bfloat16)
    denominator = jnp.sum(weights_low.astype(jnp.float32), axis=-1)
    numerator = jnp.einsum(contract, weights_low, values, preferred_element_type=jnp.float32)
    return (peak_score, denominator, numerator)


def slot_attention_kernel(
    home_ref, len_ref, incoming_hbm, cache_ref, out_ref, query_buf, sems, *, scale
):
    slot_count = cache_ref.shape[0]
    rows = incoming_hbm.shape[1]
    copies = [
        pltpu.make_async_copy(incoming_hbm.at[home_ref[i]], query_buf.at[i], sems.at[i])
        for i in range(slot_count)
    ]
    for copy in copies:
        copy.start()
    out_ref[...] = jnp.zeros(out_ref.shape, out_ref.dtype)
    for i in range(slot_count):
        home = home_ref[i]
        copies[i].wait()
        scores = (
            lax.dot_general(
                query_buf[i],
                cache_ref[i, 0],
                (((1,), (1,)), ((), ())),
                preferred_element_type=jnp.float32,
            )
            * scale
        )
        position = lax.broadcasted_iota(jnp.int32, scores.shape, 1)
        masked = jnp.where(position < len_ref[i], scores, -jnp.inf)
        peak = jnp.max(masked, axis=1, keepdims=True)
        weights = jnp.exp(masked - peak).astype(jnp.bfloat16)
        den = jnp.sum(weights.astype(jnp.float32), axis=1, keepdims=True)
        num = jnp.dot(weights, cache_ref[i, 1], preferred_element_type=jnp.float32)
        peak_low = peak.astype(jnp.bfloat16).astype(jnp.float32)
        shift = jnp.exp(peak - peak_low)
        shifted_den = den * shift
        den_high = shifted_den.astype(jnp.bfloat16).astype(jnp.float32)
        den_rest = shifted_den - den_high
        lane = lax.broadcasted_iota(jnp.int32, (rows, out_ref.shape[2]), 1)
        facts = jnp.where(
            lane == 0,
            peak_low,
            jnp.where(lane == 1, den_high, jnp.where(lane == 2, den_rest, 0.0)),
        )
        out_ref[home, :rows, :] = (num * shift).astype(out_ref.dtype)
        out_ref[home, rows:, :] = facts.astype(out_ref.dtype)


def slot_attention(home, cache_len, incoming, cache_kv, scale):
    groups, rows, width = incoming.shape
    slot_count, _, cache_size, _ = cache_kv.shape
    flops = 4 * slot_count * rows * cache_size * width
    moved = 2 * (cache_kv.size + incoming.size + 2 * groups * rows * width)
    return pl.pallas_call(
        functools.partial(slot_attention_kernel, scale=scale),
        out_shape=jax.ShapeDtypeStruct((groups, 2 * rows, width), incoming.dtype),
        in_specs=[
            pl.BlockSpec(memory_space=pltpu.SMEM),
            pl.BlockSpec(memory_space=pltpu.SMEM),
            pl.BlockSpec(memory_space=pl.ANY),
            pl.BlockSpec(memory_space=pltpu.VMEM),
        ],
        out_specs=pl.BlockSpec(memory_space=pltpu.VMEM),
        scratch_shapes=[
            pltpu.VMEM((slot_count, rows, width), incoming.dtype),
            pltpu.SemaphoreType.DMA((slot_count,)),
        ],
        cost_estimate=pl.CostEstimate(
            flops=flops, transcendentals=slot_count * rows * cache_size, bytes_accessed=moved
        ),
    )(home, cache_len, incoming, cache_kv)


def on_device(
    draft_hidden,
    q_weight,
    kv_weight,
    router_weight,
    routes,
    tree_mask,
    accepted,
    cache_kv,
    cache_len,
    slot_request,
):
    highest = lax.Precision.HIGHEST
    requests, drafts, part_width = draft_hidden.shape
    experts = q_weight.shape[0]
    head_width = q_weight.shape[2]
    head_count = head_width // HEAD_SIZE
    topk_count = routes.shape[2]
    kept_rows = accepted.shape[1]
    score_scale = HEAD_SIZE ** (-0.5)
    group_count = lax.axis_size("grp")
    group_idx = lax.axis_index("grp")
    slot_count = cache_kv.shape[0]
    cache_size = cache_kv.shape[2]

    row_pick = accepted[:, :, None] == jnp.arange(drafts, dtype=jnp.int32)[None, None, :]
    acc_part = jnp.einsum(
        "rat,rtd->rad",
        row_pick.astype(draft_hidden.dtype),
        draft_hidden,
        preferred_element_type=jnp.float32,
    ).astype(draft_hidden.dtype)
    acc_routes = jnp.sum(jnp.where(row_pick[..., None], routes[:, None], 0), axis=2)
    mask_rows = jnp.sum(jnp.where(row_pick[..., None], tree_mask[:, None], 0), axis=2)
    acc_mask = jnp.sum(jnp.where(row_pick[:, None, :, :], mask_rows[:, :, None, :], 0), axis=3)
    order = jnp.arange(kept_rows, dtype=jnp.int32)
    repeated = jnp.any(
        (accepted[:, :, None] == accepted[:, None, :]) & (order[None, None, :] < order[None, :, None]),
        axis=2,
    )
    usable_keys = (acc_mask > 0) & ~repeated[:, None, :]

    model_count = lax.axis_size("mdl")
    hidden_parts = lax.all_to_all(
        jnp.broadcast_to(acc_part[None], (model_count,) + acc_part.shape),
        "mdl",
        0,
        0,
        tiled=True,
    )
    acc_hidden = hidden_parts.transpose(1, 2, 0, 3).reshape(
        requests, kept_rows, model_count * part_width
    )

    q_sum = jnp.einsum("rad,edw->raew", acc_hidden, q_weight, preferred_element_type=jnp.float32)
    kv_sum = jnp.einsum("rtd,cdw->rtcw", acc_hidden, kv_weight, preferred_element_type=jnp.float32)
    logit_sum = jnp.einsum(
        "rad,de->rae", acc_hidden.astype(jnp.float32), router_weight, precision=highest
    )
    chosen_mask = acc_routes[..., None] == jnp.arange(experts, dtype=jnp.int32)
    chosen = jnp.sum(jnp.where(chosen_mask, logit_sum[:, :, None, :], 0.0), axis=3)
    gate_probs = jax.nn.softmax(chosen, axis=-1)
    queries = jnp.sum(jnp.where(chosen_mask[..., None], q_sum[:, :, None], 0.0), axis=3)
    queries = queries.astype(jnp.bfloat16)
    draft_keys = kv_sum[:, :, 0].astype(jnp.bfloat16)
    draft_values = kv_sum[:, :, 1].astype(jnp.bfloat16)

    tree_scores = (
        jnp.einsum("rakw,rjw->rakj", queries, draft_keys, preferred_element_type=jnp.float32)
        * score_scale
    )
    tree_peak, tree_den, tree_num = softmax_piece(
        tree_scores, usable_keys[:, :, None, :], draft_values, "rakj,rjw->rakw"
    )

    slot_table = slot_request.reshape(group_count, slot_count)
    home_of = slot_table // requests
    local_of = slot_table % requests
    mine = home_of == group_idx
    picked = jnp.sum(jnp.where(mine, local_of, 0), axis=1)
    any_mine = jnp.any(mine, axis=1)
    query_rows = queries.reshape(requests, kept_rows * topk_count, head_width)
    outgoing = jnp.where(
        any_mine[:, None, None],
        jnp.where((picked == 1)[:, None, None], query_rows[1][None], query_rows[0][None]),
        jnp.zeros((), query_rows.dtype),
    )
    incoming = lax.all_to_all(outgoing, "grp", 0, 0, tiled=True)

    my_slots = lax.dynamic_slice_in_dim(slot_request, group_idx * slot_count, slot_count)
    row_count = kept_rows * topk_count
    returning = slot_attention(my_slots // requests, cache_len, incoming, cache_kv, score_scale)
    back = lax.all_to_all(returning, "grp", 0, 0, tiled=True)
    serving = jnp.any(home_of == group_idx, axis=1)
    place = jnp.cumsum(serving.astype(jnp.int32)) - 1
    source_pick = serving[None, :] & (
        place[None, :] == jnp.arange(slot_count, dtype=jnp.int32)[:, None]
    )
    source_valid = jnp.any(source_pick, axis=1)
    source_request = jnp.sum(
        jnp.where(source_pick, jnp.sum(jnp.where(mine, local_of, 0), axis=1)[None, :], 0), axis=1
    )
    chosen_blocks = (
        jnp.einsum(
            "kd,dx->kx",
            source_pick.astype(back.dtype),
            back.reshape(group_count, -1),
            preferred_element_type=jnp.float32,
        )
        .reshape(slot_count, 2 * row_count, head_width)
    )
    back_num = chosen_blocks[:, :row_count].reshape(slot_count, kept_rows, topk_count, head_width)
    back_facts = chosen_blocks[:, row_count:, :3]
    back_peak = back_facts[..., 0].reshape(slot_count, kept_rows, topk_count)
    back_den = (back_facts[..., 1] + back_facts[..., 2]).reshape(slot_count, kept_rows, topk_count)

    matched = (
        source_valid[None, :]
        & (source_request[None, :] == jnp.arange(requests, dtype=jnp.int32)[:, None])
    )
    candidate = jnp.where(matched[:, :, None, None], back_peak[None], -jnp.inf)
    running_max = jnp.maximum(tree_peak, jnp.max(candidate, axis=1))
    rescale = jnp.exp(tree_peak - running_max)
    weight = jnp.exp(candidate - running_max[:, None])
    denominator = tree_den * rescale + jnp.sum(weight * back_den[None], axis=1)
    numerator = tree_num * rescale[..., None] + jnp.sum(
        weight[..., None] * back_num[None], axis=1
    )
    mixed = gate_probs[..., None] * numerator / denominator[..., None]
    return mixed.reshape(requests, kept_rows, topk_count, head_width).astype(jnp.bfloat16)


def solution(mesh):
    in_specs = (
        P("grp", None, "mdl"),
        P(None, None, "mdl"),
        P(None, None, "mdl"),
        P(),
        P("grp", None, None),
        P("grp", None, None),
        P("grp", None),
        P("grp", None, None, "mdl"),
        P("grp"),
        P(),
    )
    out_specs = P("grp", None, None, "mdl")
    return jax.shard_map(
        on_device, mesh=mesh, in_specs=in_specs, out_specs=out_specs, check_vma=False
    )
```

```python
import jax
import jax.numpy as jnp
import functools

from jax import lax
from jax.experimental import pallas as pl
from jax.experimental.pallas import tpu as pltpu
from jax.sharding import PartitionSpec as P

HEAD_SIZE = 128


def softmax_piece(scores, usable, values, contract):
    masked = jnp.where(usable, scores, -jnp.inf)
    peak_score = jnp.max(masked, axis=-1)
    weights_low = jnp.exp(masked - peak_score[..., None]).astype(jnp.bfloat16)
    denominator = jnp.sum(weights_low.astype(jnp.float32), axis=-1)
    numerator = jnp.einsum(contract, weights_low, values, preferred_element_type=jnp.float32)
    return (peak_score, denominator, numerator)


def slot_attention_kernel(
    home_ref, len_ref, incoming_ref, cache_hbm, out_ref, cache_ref, sems, *, scale
):
    slot_count = cache_ref.shape[0]
    rows = incoming_ref.shape[1]
    copies = [
        [
            pltpu.make_async_copy(cache_hbm.at[i, c], cache_ref.at[i, c], sems.at[i, c])
            for c in range(2)
        ]
        for i in range(slot_count)
    ]
    for pair in copies:
        for copy in pair:
            copy.start()
    out_ref[...] = jnp.zeros(out_ref.shape, out_ref.dtype)
    for i in range(slot_count):
        home = home_ref[i]
        copies[i][0].wait()
        scores = (
            lax.dot_general(
                incoming_ref[home],
                cache_ref[i, 0],
                (((1,), (1,)), ((), ())),
                preferred_element_type=jnp.float32,
            )
            * scale
        )
        position = lax.broadcasted_iota(jnp.int32, scores.shape, 1)
        masked = jnp.where(position < len_ref[i], scores, -jnp.inf)
        peak = jnp.max(masked, axis=1, keepdims=True)
        weights = jnp.exp(masked - peak).astype(jnp.bfloat16)
        den = jnp.sum(weights.astype(jnp.float32), axis=1, keepdims=True)
        copies[i][1].wait()
        num = jnp.dot(weights, cache_ref[i, 1], preferred_element_type=jnp.float32)
        peak_low = peak.astype(jnp.bfloat16).astype(jnp.float32)
        shift = jnp.exp(peak - peak_low)
        shifted_den = den * shift
        den_high = shifted_den.astype(jnp.bfloat16).astype(jnp.float32)
        den_rest = shifted_den - den_high
        lane = lax.broadcasted_iota(jnp.int32, (rows, out_ref.shape[2]), 1)
        facts = jnp.where(
            lane == 0,
            peak_low,
            jnp.where(lane == 1, den_high, jnp.where(lane == 2, den_rest, 0.0)),
        )
        out_ref[home, :rows, :] = (num * shift).astype(out_ref.dtype)
        out_ref[home, rows:, :] = facts.astype(out_ref.dtype)


def slot_attention(home, cache_len, incoming, cache_kv, scale):
    groups, rows, width = incoming.shape
    slot_count, _, cache_size, _ = cache_kv.shape
    flops = 4 * slot_count * rows * cache_size * width
    moved = 2 * (cache_kv.size + incoming.size + 2 * groups * rows * width)
    return pl.pallas_call(
        functools.partial(slot_attention_kernel, scale=scale),
        out_shape=jax.ShapeDtypeStruct((groups, 2 * rows, width), incoming.dtype),
        in_specs=[
            pl.BlockSpec(memory_space=pltpu.SMEM),
            pl.BlockSpec(memory_space=pltpu.SMEM),
            pl.BlockSpec(memory_space=pltpu.VMEM),
            pl.BlockSpec(memory_space=pl.ANY),
        ],
        out_specs=pl.BlockSpec(memory_space=pltpu.VMEM),
        scratch_shapes=[
            pltpu.VMEM(cache_kv.shape, cache_kv.dtype),
            pltpu.SemaphoreType.DMA((slot_count, 2)),
        ],
        cost_estimate=pl.CostEstimate(
            flops=flops, transcendentals=slot_count * rows * cache_size, bytes_accessed=moved
        ),
    )(home, cache_len, incoming, cache_kv)


def on_device(
    draft_hidden,
    q_weight,
    kv_weight,
    router_weight,
    routes,
    tree_mask,
    accepted,
    cache_kv,
    cache_len,
    slot_request,
):
    highest = lax.Precision.HIGHEST
    requests, drafts, part_width = draft_hidden.shape
    experts = q_weight.shape[0]
    head_width = q_weight.shape[2]
    head_count = head_width // HEAD_SIZE
    topk_count = routes.shape[2]
    kept_rows = accepted.shape[1]
    score_scale = HEAD_SIZE ** (-0.5)
    group_count = lax.axis_size("grp")
    group_idx = lax.axis_index("grp")
    slot_count = cache_kv.shape[0]
    cache_size = cache_kv.shape[2]

    row_pick = accepted[:, :, None] == jnp.arange(drafts, dtype=jnp.int32)[None, None, :]
    acc_part = jnp.einsum(
        "rat,rtd->rad",
        row_pick.astype(draft_hidden.dtype),
        draft_hidden,
        preferred_element_type=jnp.float32,
    ).astype(draft_hidden.dtype)
    acc_routes = jnp.sum(jnp.where(row_pick[..., None], routes[:, None], 0), axis=2)
    mask_rows = jnp.sum(jnp.where(row_pick[..., None], tree_mask[:, None], 0), axis=2)
    acc_mask = jnp.sum(jnp.where(row_pick[:, None, :, :], mask_rows[:, :, None, :], 0), axis=3)
    order = jnp.arange(kept_rows, dtype=jnp.int32)
    repeated = jnp.any(
        (accepted[:, :, None] == accepted[:, None, :]) & (order[None, None, :] < order[None, :, None]),
        axis=2,
    )
    usable_keys = (acc_mask > 0) & ~repeated[:, None, :]

    model_count = lax.axis_size("mdl")
    hidden_parts = lax.all_to_all(
        jnp.broadcast_to(acc_part[None], (model_count,) + acc_part.shape),
        "mdl",
        0,
        0,
        tiled=True,
    )
    acc_hidden = hidden_parts.transpose(1, 2, 0, 3).reshape(
        requests, kept_rows, model_count * part_width
    )

    q_sum = jnp.einsum("rad,edw->raew", acc_hidden, q_weight, preferred_element_type=jnp.float32)
    kv_sum = jnp.einsum("rtd,cdw->rtcw", acc_hidden, kv_weight, preferred_element_type=jnp.float32)
    logit_sum = jnp.einsum(
        "rad,de->rae", acc_hidden.astype(jnp.float32), router_weight, precision=highest
    )
    chosen_mask = acc_routes[..., None] == jnp.arange(experts, dtype=jnp.int32)
    chosen = jnp.sum(jnp.where(chosen_mask, logit_sum[:, :, None, :], 0.0), axis=3)
    gate_probs = jax.nn.softmax(chosen, axis=-1)
    queries = jnp.sum(jnp.where(chosen_mask[..., None], q_sum[:, :, None], 0.0), axis=3)
    queries = queries.astype(jnp.bfloat16)
    draft_keys = kv_sum[:, :, 0].astype(jnp.bfloat16)
    draft_values = kv_sum[:, :, 1].astype(jnp.bfloat16)

    tree_scores = (
        jnp.einsum("rakw,rjw->rakj", queries, draft_keys, preferred_element_type=jnp.float32)
        * score_scale
    )
    tree_peak, tree_den, tree_num = softmax_piece(
        tree_scores, usable_keys[:, :, None, :], draft_values, "rakj,rjw->rakw"
    )

    slot_table = slot_request.reshape(group_count, slot_count)
    home_of = slot_table // requests
    local_of = slot_table % requests
    mine = home_of == group_idx
    picked = jnp.sum(jnp.where(mine, local_of, 0), axis=1)
    any_mine = jnp.any(mine, axis=1)
    query_rows = queries.reshape(requests, kept_rows * topk_count, head_width)
    outgoing = jnp.where(
        any_mine[:, None, None],
        jnp.where((picked == 1)[:, None, None], query_rows[1][None], query_rows[0][None]),
        jnp.zeros((), query_rows.dtype),
    )
    incoming = lax.all_to_all(outgoing, "grp", 0, 0, tiled=True)

    my_slots = lax.dynamic_slice_in_dim(slot_request, group_idx * slot_count, slot_count)
    row_count = kept_rows * topk_count
    returning = slot_attention(my_slots // requests, cache_len, incoming, cache_kv, score_scale)
    back = lax.all_to_all(returning, "grp", 0, 0, tiled=True)
    serving = jnp.any(home_of == group_idx, axis=1)
    place = jnp.cumsum(serving.astype(jnp.int32)) - 1
    source_pick = serving[None, :] & (
        place[None, :] == jnp.arange(slot_count, dtype=jnp.int32)[:, None]
    )
    source_valid = jnp.any(source_pick, axis=1)
    source_request = jnp.sum(
        jnp.where(source_pick, jnp.sum(jnp.where(mine, local_of, 0), axis=1)[None, :], 0), axis=1
    )
    chosen_blocks = (
        jnp.einsum(
            "kd,dx->kx",
            source_pick.astype(back.dtype),
            back.reshape(group_count, -1),
            preferred_element_type=jnp.float32,
        )
        .reshape(slot_count, 2 * row_count, head_width)
    )
    back_num = chosen_blocks[:, :row_count].reshape(slot_count, kept_rows, topk_count, head_width)
    back_facts = chosen_blocks[:, row_count:, :3]
    back_peak = back_facts[..., 0].reshape(slot_count, kept_rows, topk_count)
    back_den = (back_facts[..., 1] + back_facts[..., 2]).reshape(slot_count, kept_rows, topk_count)

    matched = (
        source_valid[None, :]
        & (source_request[None, :] == jnp.arange(requests, dtype=jnp.int32)[:, None])
    )
    candidate = jnp.where(matched[:, :, None, None], back_peak[None], -jnp.inf)
    running_max = jnp.maximum(tree_peak, jnp.max(candidate, axis=1))
    rescale = jnp.exp(tree_peak - running_max)
    weight = jnp.exp(candidate - running_max[:, None])
    denominator = tree_den * rescale + jnp.sum(weight * back_den[None], axis=1)
    numerator = tree_num * rescale[..., None] + jnp.sum(
        weight[..., None] * back_num[None], axis=1
    )
    mixed = gate_probs[..., None] * numerator / denominator[..., None]
    return mixed.reshape(requests, kept_rows, topk_count, head_width).astype(jnp.bfloat16)


def solution(mesh):
    in_specs = (
        P("grp", None, "mdl"),
        P(None, None, "mdl"),
        P(None, None, "mdl"),
        P(),
        P("grp", None, None),
        P("grp", None, None),
        P("grp", None),
        P("grp", None, None, "mdl"),
        P("grp"),
        P(),
    )
    out_specs = P("grp", None, None, "mdl")
    return jax.shard_map(
        on_device, mesh=mesh, in_specs=in_specs, out_specs=out_specs, check_vma=False
    )
```

```python
import jax
import jax.numpy as jnp
import functools

from jax import lax
from jax.experimental import pallas as pl
from jax.experimental.pallas import tpu as pltpu
from jax.sharding import PartitionSpec as P

HEAD_SIZE = 128


def softmax_piece(scores, usable, values, contract):
    masked = jnp.where(usable, scores, -jnp.inf)
    peak_score = jnp.max(masked, axis=-1)
    weights_low = jnp.exp(masked - peak_score[..., None]).astype(jnp.bfloat16)
    denominator = jnp.sum(weights_low.astype(jnp.float32), axis=-1)
    numerator = jnp.einsum(contract, weights_low, values, preferred_element_type=jnp.float32)
    return (peak_score, denominator, numerator)


def slot_attention_kernel(home_ref, len_ref, incoming_ref, cache_ref, out_ref, *, scale):
    slot_count = cache_ref.shape[0]
    rows = incoming_ref.shape[1]
    out_ref[...] = jnp.zeros(out_ref.shape, out_ref.dtype)
    for i in range(slot_count):
        home = home_ref[i]
        scores = (
            lax.dot_general(
                incoming_ref[home],
                cache_ref[i, 0],
                (((1,), (1,)), ((), ())),
                preferred_element_type=jnp.float32,
            )
            * scale
        )
        position = lax.broadcasted_iota(jnp.int32, scores.shape, 1)
        masked = jnp.where(position < len_ref[i], scores, -jnp.inf)
        peak = jnp.max(masked, axis=1, keepdims=True)
        weights = jnp.exp(masked - peak).astype(jnp.bfloat16)
        den = jnp.sum(weights.astype(jnp.float32), axis=1, keepdims=True)
        num = jnp.dot(weights, cache_ref[i, 1], preferred_element_type=jnp.float32)
        peak_low = peak.astype(jnp.bfloat16).astype(jnp.float32)
        shift = jnp.exp(peak - peak_low)
        shifted_den = den * shift
        den_high = shifted_den.astype(jnp.bfloat16).astype(jnp.float32)
        den_rest = shifted_den - den_high
        lane = lax.broadcasted_iota(jnp.int32, (rows, out_ref.shape[2]), 1)
        facts = jnp.where(
            lane == 0,
            peak_low,
            jnp.where(lane == 1, den_high, jnp.where(lane == 2, den_rest, 0.0)),
        )
        out_ref[home, :rows, :] = (num * shift).astype(out_ref.dtype)
        out_ref[home, rows:, :] = facts.astype(out_ref.dtype)


def slot_attention(home, cache_len, incoming, cache_kv, scale):
    groups, rows, width = incoming.shape
    slot_count, _, cache_size, _ = cache_kv.shape
    flops = 4 * slot_count * rows * cache_size * width
    moved = 2 * (cache_kv.size + incoming.size + 2 * groups * rows * width)
    return pl.pallas_call(
        functools.partial(slot_attention_kernel, scale=scale),
        out_shape=jax.ShapeDtypeStruct((groups, 2 * rows, width), incoming.dtype),
        in_specs=[
            pl.BlockSpec(memory_space=pltpu.SMEM),
            pl.BlockSpec(memory_space=pltpu.SMEM),
            pl.BlockSpec(memory_space=pltpu.VMEM),
            pl.BlockSpec(memory_space=pltpu.VMEM),
        ],
        out_specs=pl.BlockSpec(memory_space=pltpu.VMEM),
        cost_estimate=pl.CostEstimate(
            flops=flops, transcendentals=slot_count * rows * cache_size, bytes_accessed=moved
        ),
    )(home, cache_len, incoming, cache_kv)


def on_device(
    draft_hidden,
    q_weight,
    kv_weight,
    router_weight,
    routes,
    tree_mask,
    accepted,
    cache_kv,
    cache_len,
    slot_request,
):
    highest = lax.Precision.HIGHEST
    requests, drafts, part_width = draft_hidden.shape
    experts = q_weight.shape[0]
    head_width = q_weight.shape[2]
    head_count = head_width // HEAD_SIZE
    topk_count = routes.shape[2]
    kept_rows = accepted.shape[1]
    score_scale = HEAD_SIZE ** (-0.5)
    group_count = lax.axis_size("grp")
    group_idx = lax.axis_index("grp")
    slot_count = cache_kv.shape[0]
    cache_size = cache_kv.shape[2]

    row_pick = accepted[:, :, None] == jnp.arange(drafts, dtype=jnp.int32)[None, None, :]
    acc_part = jnp.einsum(
        "rat,rtd->rad",
        row_pick.astype(draft_hidden.dtype),
        draft_hidden,
        preferred_element_type=jnp.float32,
    ).astype(draft_hidden.dtype)
    acc_routes = jnp.sum(jnp.where(row_pick[..., None], routes[:, None], 0), axis=2)
    mask_rows = jnp.sum(jnp.where(row_pick[..., None], tree_mask[:, None], 0), axis=2)
    acc_mask = jnp.sum(jnp.where(row_pick[:, None, :, :], mask_rows[:, :, None, :], 0), axis=3)
    order = jnp.arange(kept_rows, dtype=jnp.int32)
    repeated = jnp.any(
        (accepted[:, :, None] == accepted[:, None, :]) & (order[None, None, :] < order[None, :, None]),
        axis=2,
    )
    usable_keys = (acc_mask > 0) & ~repeated[:, None, :]

    model_count = lax.axis_size("mdl")
    hidden_parts = lax.all_to_all(
        jnp.broadcast_to(acc_part[None], (model_count,) + acc_part.shape),
        "mdl",
        0,
        0,
        tiled=True,
    )
    acc_hidden = hidden_parts.transpose(1, 2, 0, 3).reshape(
        requests, kept_rows, model_count * part_width
    )

    q_sum = jnp.einsum("rad,edw->raew", acc_hidden, q_weight, preferred_element_type=jnp.float32)
    kv_sum = jnp.einsum("rtd,cdw->rtcw", acc_hidden, kv_weight, preferred_element_type=jnp.float32)
    logit_sum = jnp.einsum(
        "rad,de->rae", acc_hidden.astype(jnp.float32), router_weight, precision=highest
    )
    chosen_mask = acc_routes[..., None] == jnp.arange(experts, dtype=jnp.int32)
    chosen = jnp.sum(jnp.where(chosen_mask, logit_sum[:, :, None, :], 0.0), axis=3)
    gate_probs = jax.nn.softmax(chosen, axis=-1)
    queries = jnp.sum(jnp.where(chosen_mask[..., None], q_sum[:, :, None], 0.0), axis=3)
    queries = queries.astype(jnp.bfloat16)
    draft_keys = kv_sum[:, :, 0].astype(jnp.bfloat16)
    draft_values = kv_sum[:, :, 1].astype(jnp.bfloat16)

    tree_scores = (
        jnp.einsum("rakw,rjw->rakj", queries, draft_keys, preferred_element_type=jnp.float32)
        * score_scale
    )
    tree_peak, tree_den, tree_num = softmax_piece(
        tree_scores, usable_keys[:, :, None, :], draft_values, "rakj,rjw->rakw"
    )

    slot_table = slot_request.reshape(group_count, slot_count)
    home_of = slot_table // requests
    local_of = slot_table % requests
    mine = home_of == group_idx
    picked = jnp.sum(jnp.where(mine, local_of, 0), axis=1)
    any_mine = jnp.any(mine, axis=1)
    query_rows = queries.reshape(requests, kept_rows * topk_count, head_width)
    outgoing = jnp.where(
        any_mine[:, None, None],
        jnp.where((picked == 1)[:, None, None], query_rows[1][None], query_rows[0][None]),
        jnp.zeros((), query_rows.dtype),
    )
    incoming = lax.all_to_all(outgoing, "grp", 0, 0, tiled=True)

    my_slots = lax.dynamic_slice_in_dim(slot_request, group_idx * slot_count, slot_count)
    row_count = kept_rows * topk_count
    returning = slot_attention(my_slots // requests, cache_len, incoming, cache_kv, score_scale)
    back = lax.all_to_all(returning, "grp", 0, 0, tiled=True)
    late_home, late_local, _ = lax.optimization_barrier((home_of, local_of, returning))
    mine = late_home == group_idx
    local_of = late_local
    serving = jnp.any(mine, axis=1)
    place = jnp.cumsum(serving.astype(jnp.int32)) - 1
    source_pick = serving[None, :] & (
        place[None, :] == jnp.arange(slot_count, dtype=jnp.int32)[:, None]
    )
    source_valid = jnp.any(source_pick, axis=1)
    source_request = jnp.sum(
        jnp.where(source_pick, jnp.sum(jnp.where(mine, local_of, 0), axis=1)[None, :], 0), axis=1
    )
    source_index = jnp.sum(
        jnp.where(source_pick, jnp.arange(group_count, dtype=jnp.int32)[None, :], 0), axis=1
    )
    chosen_blocks = jnp.stack(
        [lax.dynamic_index_in_dim(back, source_index[k], 0, keepdims=False) for k in range(slot_count)]
    ).astype(jnp.float32)
    back_num = chosen_blocks[:, :row_count].reshape(slot_count, kept_rows, topk_count, head_width)
    back_facts = chosen_blocks[:, row_count:, :3]
    back_peak = back_facts[..., 0].reshape(slot_count, kept_rows, topk_count)
    back_den = (back_facts[..., 1] + back_facts[..., 2]).reshape(slot_count, kept_rows, topk_count)

    matched = (
        source_valid[None, :]
        & (source_request[None, :] == jnp.arange(requests, dtype=jnp.int32)[:, None])
    )
    candidate = jnp.where(matched[:, :, None, None], back_peak[None], -jnp.inf)
    running_max = jnp.maximum(tree_peak, jnp.max(candidate, axis=1))
    rescale = jnp.exp(tree_peak - running_max)
    weight = jnp.exp(candidate - running_max[:, None])
    denominator = tree_den * rescale + jnp.sum(weight * back_den[None], axis=1)
    numerator = tree_num * rescale[..., None] + jnp.sum(
        weight[..., None] * back_num[None], axis=1
    )
    mixed = gate_probs[..., None] * numerator / denominator[..., None]
    return mixed.reshape(requests, kept_rows, topk_count, head_width).astype(jnp.bfloat16)


def solution(mesh):
    in_specs = (
        P("grp", None, "mdl"),
        P(None, None, "mdl"),
        P(None, None, "mdl"),
        P(),
        P("grp", None, None),
        P("grp", None, None),
        P("grp", None),
        P("grp", None, None, "mdl"),
        P("grp"),
        P(),
    )
    out_specs = P("grp", None, None, "mdl")
    return jax.shard_map(
        on_device, mesh=mesh, in_specs=in_specs, out_specs=out_specs, check_vma=False
    )
```

```python
import jax
import jax.numpy as jnp
import functools

from jax import lax
from jax.experimental import pallas as pl
from jax.experimental.pallas import tpu as pltpu
from jax.sharding import PartitionSpec as P

HEAD_SIZE = 128


def softmax_piece(scores, usable, values, contract):
    masked = jnp.where(usable, scores, -jnp.inf)
    peak_score = jnp.max(masked, axis=-1)
    weights_low = jnp.exp(masked - peak_score[..., None]).astype(jnp.bfloat16)
    denominator = jnp.sum(weights_low.astype(jnp.float32), axis=-1)
    numerator = jnp.einsum(contract, weights_low, values, preferred_element_type=jnp.float32)
    return (peak_score, denominator, numerator)


def slot_attention_kernel(home_ref, len_ref, incoming_ref, cache_ref, out_ref, *, scale):
    slot_count = cache_ref.shape[0]
    rows = incoming_ref.shape[1]
    out_ref[...] = jnp.zeros(out_ref.shape, out_ref.dtype)
    for i in range(slot_count):
        home = home_ref[i]
        scores = (
            lax.dot_general(
                incoming_ref[home],
                cache_ref[i, 0],
                (((1,), (1,)), ((), ())),
                preferred_element_type=jnp.float32,
            )
            * scale
        )
        position = lax.broadcasted_iota(jnp.int32, scores.shape, 1)
        masked = jnp.where(position < len_ref[i], scores, -jnp.inf)
        peak = jnp.max(masked, axis=1, keepdims=True)
        weights = jnp.exp(masked - peak).astype(jnp.bfloat16)
        den = jnp.sum(weights.astype(jnp.float32), axis=1, keepdims=True)
        num = jnp.dot(weights, cache_ref[i, 1], preferred_element_type=jnp.float32)
        peak_low = peak.astype(jnp.bfloat16).astype(jnp.float32)
        shift = jnp.exp(peak - peak_low)
        shifted_den = den * shift
        den_high = shifted_den.astype(jnp.bfloat16).astype(jnp.float32)
        den_rest = shifted_den - den_high
        lane = lax.broadcasted_iota(jnp.int32, (rows, out_ref.shape[2]), 1)
        facts = jnp.where(
            lane == 0,
            peak_low,
            jnp.where(lane == 1, den_high, jnp.where(lane == 2, den_rest, 0.0)),
        )
        out_ref[home, :rows, :] = (num * shift).astype(out_ref.dtype)
        out_ref[home, rows:, :] = facts.astype(out_ref.dtype)


def slot_attention(home, cache_len, incoming, cache_kv, scale):
    groups, rows, width = incoming.shape
    slot_count, _, cache_size, _ = cache_kv.shape
    flops = 4 * slot_count * rows * cache_size * width
    moved = 2 * (cache_kv.size + incoming.size + 2 * groups * rows * width)
    return pl.pallas_call(
        functools.partial(slot_attention_kernel, scale=scale),
        out_shape=jax.ShapeDtypeStruct((groups, 2 * rows, width), incoming.dtype),
        in_specs=[
            pl.BlockSpec(memory_space=pltpu.SMEM),
            pl.BlockSpec(memory_space=pltpu.SMEM),
            pl.BlockSpec(memory_space=pltpu.VMEM),
            pl.BlockSpec(memory_space=pltpu.VMEM),
        ],
        out_specs=pl.BlockSpec(memory_space=pltpu.VMEM),
        compiler_params=pltpu.CompilerParams(vmem_limit_bytes=16 * 1024 * 1024),
        cost_estimate=pl.CostEstimate(
            flops=flops, transcendentals=slot_count * rows * cache_size, bytes_accessed=moved
        ),
    )(home, cache_len, incoming, cache_kv)


def on_device(
    draft_hidden,
    q_weight,
    kv_weight,
    router_weight,
    routes,
    tree_mask,
    accepted,
    cache_kv,
    cache_len,
    slot_request,
):
    highest = lax.Precision.HIGHEST
    requests, drafts, part_width = draft_hidden.shape
    experts = q_weight.shape[0]
    head_width = q_weight.shape[2]
    head_count = head_width // HEAD_SIZE
    topk_count = routes.shape[2]
    kept_rows = accepted.shape[1]
    score_scale = HEAD_SIZE ** (-0.5)
    group_count = lax.axis_size("grp")
    group_idx = lax.axis_index("grp")
    slot_count = cache_kv.shape[0]
    cache_size = cache_kv.shape[2]

    row_pick = accepted[:, :, None] == jnp.arange(drafts, dtype=jnp.int32)[None, None, :]
    acc_part = jnp.einsum(
        "rat,rtd->rad",
        row_pick.astype(draft_hidden.dtype),
        draft_hidden,
        preferred_element_type=jnp.float32,
    ).astype(draft_hidden.dtype)
    acc_routes = jnp.sum(jnp.where(row_pick[..., None], routes[:, None], 0), axis=2)
    mask_rows = jnp.sum(jnp.where(row_pick[..., None], tree_mask[:, None], 0), axis=2)
    acc_mask = jnp.sum(jnp.where(row_pick[:, None, :, :], mask_rows[:, :, None, :], 0), axis=3)
    order = jnp.arange(kept_rows, dtype=jnp.int32)
    repeated = jnp.any(
        (accepted[:, :, None] == accepted[:, None, :]) & (order[None, None, :] < order[None, :, None]),
        axis=2,
    )
    usable_keys = (acc_mask > 0) & ~repeated[:, None, :]

    model_count = lax.axis_size("mdl")
    hidden_parts = lax.all_to_all(
        jnp.broadcast_to(acc_part[None], (model_count,) + acc_part.shape),
        "mdl",
        0,
        0,
        tiled=True,
    )
    acc_hidden = hidden_parts.transpose(1, 2, 0, 3).reshape(
        requests, kept_rows, model_count * part_width
    )

    q_sum = jnp.einsum("rad,edw->raew", acc_hidden, q_weight, preferred_element_type=jnp.float32)
    kv_sum = jnp.einsum("rtd,cdw->rtcw", acc_hidden, kv_weight, preferred_element_type=jnp.float32)
    logit_sum = jnp.einsum(
        "rad,de->rae", acc_hidden.astype(jnp.float32), router_weight, precision=highest
    )
    chosen_mask = acc_routes[..., None] == jnp.arange(experts, dtype=jnp.int32)
    chosen = jnp.sum(jnp.where(chosen_mask, logit_sum[:, :, None, :], 0.0), axis=3)
    gate_probs = jax.nn.softmax(chosen, axis=-1)
    queries = jnp.sum(jnp.where(chosen_mask[..., None], q_sum[:, :, None], 0.0), axis=3)
    queries = queries.astype(jnp.bfloat16)
    draft_keys = kv_sum[:, :, 0].astype(jnp.bfloat16)
    draft_values = kv_sum[:, :, 1].astype(jnp.bfloat16)

    tree_scores = (
        jnp.einsum("rakw,rjw->rakj", queries, draft_keys, preferred_element_type=jnp.float32)
        * score_scale
    )
    tree_peak, tree_den, tree_num = softmax_piece(
        tree_scores, usable_keys[:, :, None, :], draft_values, "rakj,rjw->rakw"
    )

    slot_table = slot_request.reshape(group_count, slot_count)
    home_of = slot_table // requests
    local_of = slot_table % requests
    mine = home_of == group_idx
    picked = jnp.sum(jnp.where(mine, local_of, 0), axis=1)
    any_mine = jnp.any(mine, axis=1)
    query_rows = queries.reshape(requests, kept_rows * topk_count, head_width)
    outgoing = jnp.where(
        any_mine[:, None, None],
        jnp.where((picked == 1)[:, None, None], query_rows[1][None], query_rows[0][None]),
        jnp.zeros((), query_rows.dtype),
    )
    incoming = lax.all_to_all(outgoing, "grp", 0, 0, tiled=True)

    my_slots = lax.dynamic_slice_in_dim(slot_request, group_idx * slot_count, slot_count)
    row_count = kept_rows * topk_count
    returning = slot_attention(my_slots // requests, cache_len, incoming, cache_kv, score_scale)
    back = lax.all_to_all(returning, "grp", 0, 0, tiled=True)
    serving = jnp.any(home_of == group_idx, axis=1)
    place = jnp.cumsum(serving.astype(jnp.int32)) - 1
    source_pick = serving[None, :] & (
        place[None, :] == jnp.arange(slot_count, dtype=jnp.int32)[:, None]
    )
    source_valid = jnp.any(source_pick, axis=1)
    source_request = jnp.sum(
        jnp.where(source_pick, jnp.sum(jnp.where(mine, local_of, 0), axis=1)[None, :], 0), axis=1
    )
    chosen_blocks = (
        jnp.einsum(
            "kd,dx->kx",
            source_pick.astype(back.dtype),
            back.reshape(group_count, -1),
            preferred_element_type=jnp.float32,
        )
        .reshape(slot_count, 2 * row_count, head_width)
    )
    back_num = chosen_blocks[:, :row_count].reshape(slot_count, kept_rows, topk_count, head_width)
    back_facts = chosen_blocks[:, row_count:, :3]
    back_peak = back_facts[..., 0].reshape(slot_count, kept_rows, topk_count)
    back_den = (back_facts[..., 1] + back_facts[..., 2]).reshape(slot_count, kept_rows, topk_count)

    matched = (
        source_valid[None, :]
        & (source_request[None, :] == jnp.arange(requests, dtype=jnp.int32)[:, None])
    )
    candidate = jnp.where(matched[:, :, None, None], back_peak[None], -jnp.inf)
    running_max = jnp.maximum(tree_peak, jnp.max(candidate, axis=1))
    rescale = jnp.exp(tree_peak - running_max)
    weight = jnp.exp(candidate - running_max[:, None])
    denominator = tree_den * rescale + jnp.sum(weight * back_den[None], axis=1)
    numerator = tree_num * rescale[..., None] + jnp.sum(
        weight[..., None] * back_num[None], axis=1
    )
    mixed = gate_probs[..., None] * numerator / denominator[..., None]
    return mixed.reshape(requests, kept_rows, topk_count, head_width).astype(jnp.bfloat16)


def solution(mesh):
    in_specs = (
        P("grp", None, "mdl"),
        P(None, None, "mdl"),
        P(None, None, "mdl"),
        P(),
        P("grp", None, None),
        P("grp", None, None),
        P("grp", None),
        P("grp", None, None, "mdl"),
        P("grp"),
        P(),
    )
    out_specs = P("grp", None, None, "mdl")
    return jax.shard_map(
        on_device, mesh=mesh, in_specs=in_specs, out_specs=out_specs, check_vma=False
    )
```
